256 devices in a mesh: seq: 32 (over z, x), tp: 8 (over y, core).
Axes of the slice: x: 4, y: 4, z: 8, core: 2. Of those that a mesh axis runs over, the one named last changes fastest.
Arguments:
- inputs: bfloat16 [4096, 8192], P('seq', 'tp'), may hold values from -6 to 6
- input_proj: bfloat16 [4096, 2048], P('seq', 'tp'), may hold values from -0.59765625 to 0.59765625
- readout: bfloat16 [4096, 2048], P('seq', 'tp'), may hold values from -0.59765625 to 0.59765625
- step_size: float32 [4096, 128], P('seq', 'tp'), may hold values from 0.001 to 0.1
- decay_rate: float32 [128], P('tp'), may hold values from 0.002 to 4
- out_grad: bfloat16 [4096, 8192], P('seq', 'tp'), may hold values from -6 to 6
Outputs:
- grad_inputs: bfloat16 [4096, 8192], P('seq', 'tp')
- grad_proj: bfloat16 [4096, 2048], P('seq', 'tp')
- grad_read: bfloat16 [4096, 2048], P('seq', 'tp')
- grad_step: float32 [4096, 128], P(('seq', 'tp'))
The draws below stay inside these ranges and needn't reach their ends.
All inputs are finite; a program needn't handle non-finite values.
Results may differ from the reference program's by a relative error of at most 0.001.
Values sent between devices are 32-bit elements; how exact they have to be, the bound alone decides.
No kernel may reach another device: no remote copies, remote signals or barrier semaphores. Data moves between devices by JAX's collectives and lax.ppermute only.
A program may use at most 192 MiB of HBM per device.

```python
import math
import jax
import jax.numpy as jnp
from jax import lax

HEADS = 128
GROUPS = 8
HEAD_DIM = 64
D_STATE = 256
SPAN = 128
TOKENS = 4096


def levels(own_key, dims, cuts, low, top_value):
    gain = 1.0
    for axis_at, blocks in cuts:
        draws = jax.random.uniform(jax.random.fold_in(jax.random.fold_in(own_key, 6), axis_at), (blocks,), jnp.float32, low / len(cuts), top_value / len(cuts))
        gain = gain * jnp.repeat(jnp.exp(draws), dims[axis_at] // blocks).reshape((-1,) + (1,) * (len(dims) - 1 - axis_at))
    return gain


def centred(own_key, dims, deviation, most, shards=(), held_as=jnp.bfloat16):
    result = deviation * jax.random.normal(own_key, dims, jnp.float32)
    if shards:
        result = result * levels(own_key, dims, shards, -0.22, 0.18)
    return jnp.clip(result, -most, most).astype(held_as)


def setup_inputs(seed: int = 0) -> dict:
    arg_keys = jax.random.split(jax.random.key(seed), 7)
    inputs = centred(arg_keys[0], (TOKENS, HEADS * HEAD_DIM), 1.0, 6.0, ((0, 32), (1, 8)))
    input_proj = centred(arg_keys[1], (TOKENS, GROUPS * D_STATE), 0.1, 0.59765625, ((0, 32), (1, 8)))
    readout = centred(arg_keys[2], (TOKENS, GROUPS * D_STATE), 0.1, 0.59765625, ((0, 32), (1, 8)))
    step_size = jnp.clip(jnp.exp(math.log(0.1) - 4.6051702 * jax.random.uniform(arg_keys[3], (TOKENS, HEADS), jnp.float32) ** levels(arg_keys[3], (TOKENS, HEADS), ((0, 32), (1, 8)), -0.2, 0.2)), 0.001, 0.1)
    decay_rate = jnp.clip(jnp.exp(math.log(4.0) - 7.6009024 * jax.random.uniform(arg_keys[4], (HEADS,), jnp.float32) ** levels(arg_keys[4], (HEADS,), ((0, 8),), -0.2, 0.2)), 0.002, 4.0)
    out_grad = centred(arg_keys[5], (TOKENS, HEADS * HEAD_DIM), 1.0, 6.0, ((0, 32), (1, 8)))
    return dict(inputs=inputs, input_proj=input_proj, readout=readout, step_size=step_size, decay_rate=decay_rate, out_grad=out_grad)


precise = lax.Precision.HIGHEST


def summarize(inputs, out_grad, input_proj, readout, step_size, decay_rate):
    cumulative = jnp.cumsum(-decay_rate[None] * step_size, axis=0)
    totals = cumulative[-1]
    to_end = jnp.exp(totals[None] - cumulative) * step_size
    forward = jnp.einsum('qghp,qgn->ghnp', inputs * to_end[..., None], input_proj, precision=precise)
    from_start = jnp.exp(cumulative)
    backward = jnp.einsum('qghp,qgn->ghnp', out_grad * from_start[..., None], readout, precision=precise)
    return totals, forward, backward


def span_backward(inputs, out_grad, input_proj, readout, step_size, decay_rate, state_in, grad_in):
    length = inputs.shape[0]
    position = jnp.arange(length)
    causal = (position[:, None] >= position[None, :]).astype(jnp.float32)
    strictly = (position[:, None] < position[None, :]).astype(jnp.float32)
    cumulative = jnp.cumsum(-decay_rate[None] * step_size, axis=0)
    totals = cumulative[-1]
    spread = cumulative[:, None] - cumulative[None, :]
    decays = jnp.exp(jnp.minimum(spread, 0.0)) * causal[:, :, None, None]
    to_end = jnp.exp(totals[None] - cumulative)
    from_start = jnp.exp(cumulative)
    state_match = jnp.einsum('ugn,sgn->usg', readout, input_proj, precision=precise)
    grad_match = jnp.einsum('ughp,sghp->usgh', out_grad, inputs, precision=precise)
    mix_input = decays * state_match[..., None]
    back_b = jnp.einsum('ghnp,sgn->sghp', grad_in, input_proj, precision=precise)
    vector = jnp.einsum('usgh,ughp->sghp', mix_input, out_grad, precision=precise) + to_end[..., None] * back_b
    grad_inputs = step_size[..., None] * vector
    direct = jnp.sum(inputs * vector, axis=-1)
    mix_state = decays * grad_match * step_size[None]
    back_x = jnp.einsum('ghnp,sghp->sghn', grad_in, inputs, precision=precise)
    grad_proj = jnp.einsum('usgh,ugn->sgn', mix_state, readout, precision=precise) + jnp.einsum('sgh,sghn->sgn', step_size * to_end, back_x, precision=precise)
    state_out = jnp.einsum('ghnp,ughp->ughn', state_in, out_grad, precision=precise)
    grad_read = jnp.einsum('usgh,sgn->ugn', mix_state, input_proj, precision=precise) + jnp.einsum('ugh,ughn->ugn', from_start, state_out, precision=precise)
    weights = mix_state * state_match[..., None]
    exclusive = jnp.cumsum(weights, axis=1) - weights
    paired = jnp.sum(exclusive * causal[:, :, None, None], axis=0)
    from_init = from_start * jnp.einsum('ugn,ughn->ugh', readout, state_out, precision=precise)
    suffixes = jnp.einsum('ut,ugh->tgh', causal, from_init, precision=precise)
    from_tail = to_end * step_size * jnp.sum(inputs * back_b, axis=-1)
    prefixes = jnp.einsum('st,sgh->tgh', strictly, from_tail, precision=precise)
    constant = jnp.exp(totals) * jnp.sum(grad_in * state_in, axis=(2, 3))
    grad_log = paired + suffixes + prefixes + constant[None]
    grad_step = direct - decay_rate[None] * grad_log
    return grad_inputs, grad_proj, grad_read, grad_step


def combine(earlier, later):
    return (earlier[0] + later[0], jnp.exp(later[0])[..., None, None] * earlier[1] + later[1])


def span_prefix(log_sums, states, reverse):
    initial = (jnp.zeros_like(log_sums[0]), jnp.zeros_like(states[0]))

    def advance(carried, element):
        return combine(carried, element), carried

    return lax.scan(advance, initial, (log_sums, states), reverse=reverse)


def to_spans(inputs, out_grad, input_proj, readout, step_size, group_count, state_dim, head_dim, span_len):
    span_count = inputs.shape[0] // span_len
    head_count = step_size.shape[1] // group_count
    return (inputs.reshape(span_count, span_len, group_count, head_count, head_dim),
            out_grad.reshape(span_count, span_len, group_count, head_count, head_dim),
            input_proj.reshape(span_count, span_len, group_count, state_dim),
            readout.reshape(span_count, span_len, group_count, state_dim),
            step_size.reshape(span_count, span_len, group_count, head_count))


def summaries(blocks, rate_rows):
    def summarize_one(element):
        return summarize(element[0].astype(jnp.float32), element[1].astype(jnp.float32),
                         element[2].astype(jnp.float32), element[3].astype(jnp.float32),
                         element[4], rate_rows)

    return lax.map(summarize_one, blocks)


def apply_backward(blocks, rate_rows, state_ins, grad_ins):
    def backward_one(element):
        return span_backward(element[0].astype(jnp.float32), element[1].astype(jnp.float32),
                             element[2].astype(jnp.float32), element[3].astype(jnp.float32),
                             element[4], rate_rows, element[5], element[6])

    gradients = lax.map(backward_one, blocks + (state_ins, grad_ins))
    tokens = gradients[0].shape[0] * gradients[0].shape[1]
    return tuple(item_grad.reshape(tokens, -1) for item_grad in gradients)


def by_group(source, columns):
    return source.reshape(source.shape[0], GROUPS, columns).transpose(1, 0, 2)


def from_groups(source):
    return source.transpose(1, 0, 2).reshape(source.shape[1], -1)


def reference(inputs, input_proj, readout, step_size, decay_rate, out_grad):
    per_group = HEADS // GROUPS

    def group_job(element):
        blocks = to_spans(element[0], element[5], element[1], element[2], element[3], 1, D_STATE, HEAD_DIM, SPAN)
        rate_rows = element[4].reshape(1, per_group)
        totals, forward, backward = summaries(blocks, rate_rows)
        ignored_a, (log_before, state_ins) = span_prefix(totals, forward, False)
        ignored_b, (log_after, grad_ins) = span_prefix(totals, backward, True)
        return apply_backward(blocks, rate_rows, state_ins, grad_ins)

    results = lax.map(group_job, (by_group(inputs, per_group * HEAD_DIM), by_group(input_proj, D_STATE),
                                  by_group(readout, D_STATE), by_group(step_size, per_group),
                                  decay_rate.reshape(GROUPS, per_group), by_group(out_grad, per_group * HEAD_DIM)))
    grad_inputs = from_groups(results[0]).astype(jnp.bfloat16)
    grad_proj = from_groups(results[1]).astype(jnp.bfloat16)
    grad_read = from_groups(results[2]).astype(jnp.bfloat16)
    grad_step = from_groups(results[3])
    return (grad_inputs, grad_proj, grad_read, grad_step)
```

```python
import jax
import jax.numpy as jnp
from jax import lax
from jax.sharding import PartitionSpec as P

HEAD_DIM = 64
D_STATE = 256
SPAN = 128


precise = lax.Precision.HIGHEST


def prefix(part, axis, combine, identity, reverse):
    count = lax.axis_size(axis)
    place = lax.axis_index(axis)
    ahead = count - 1 - place if reverse else place
    gathered = jax.tree.map(lambda a: lax.all_gather(a, axis), part)
    state = jax.tree.map(lambda a, e: jnp.zeros_like(a) + jnp.asarray(e, a.dtype), part, identity)

    def one(turn, state):
        source = count - 1 - turn if reverse else turn
        return combine(
            state, jax.tree.map(lambda a: lax.dynamic_index_in_dim(a, source, 0, False), gathered)
        )

    return lax.fori_loop(0, ahead, one, state)


def seq_scan(device_log, device_fwd, device_bwd, axis):
    count = lax.axis_size(axis)
    place = lax.axis_index(axis)
    logs = lax.all_gather(device_log, axis).reshape(count, -1)
    heads = logs.shape[1]
    stacked = jnp.stack([device_fwd, device_bwd])
    shape = stacked.shape
    combos = 2 * heads
    flat = stacked.reshape(count, -1)
    pieces = lax.all_to_all(flat, axis, 0, 0, tiled=True)
    if combos % count == 0:
        per = combos // count
        held = place * per + jnp.arange(per)
    else:
        per = 1
        held = (place // (count // combos))[None]
    pieces = pieces.reshape(count, per, -1)
    chosen = jnp.take(logs, held % heads, axis=1)
    position = jnp.arange(count)
    low = jnp.minimum(position[:, None], position[None, :])
    high = jnp.maximum(position[:, None], position[None, :])
    between = ((position[None, None, :] > low[..., None]) & (position[None, None, :] < high[..., None]))
    exponent = jnp.einsum("ijm,mc->cij", between.astype(jnp.float32), chosen, precision=precise)
    before = (position[None, :] < position[:, None])
    after = (position[None, :] > position[:, None])
    mask = jnp.where((held < heads)[:, None, None], before[None], after[None])
    weights = jnp.where(mask, jnp.exp(exponent), 0.0)
    scanned = jnp.einsum("cij,jcx->icx", weights, pieces, precision=precise)
    back = lax.all_to_all(scanned.reshape(count, -1), axis, 0, 0, tiled=True)
    back = back.reshape(shape)
    return back[0], back[1]


def summarize(inputs, out_grad, input_proj, readout, step_size, decay_rate):
    cumulative = jnp.cumsum(-decay_rate[None] * step_size, axis=0)
    totals = cumulative[-1]
    to_end = jnp.exp(totals[None] - cumulative) * step_size
    forward = jnp.einsum(
        "qghp,qgn->ghnp",
        inputs.astype(jnp.float32) * to_end[..., None],
        input_proj.astype(jnp.float32),
        precision=precise,
    )
    from_start = jnp.exp(cumulative)
    backward = jnp.einsum(
        "qghp,qgn->ghnp",
        out_grad.astype(jnp.float32) * from_start[..., None],
        readout.astype(jnp.float32),
        precision=precise,
    )
    return (totals, forward, backward)


def span_backward(
    inputs_raw, out_raw, proj_raw, read_raw, step_size, decay_rate, state_in, grad_in
):
    inputs = inputs_raw.astype(jnp.float32)
    out_grad = out_raw.astype(jnp.float32)
    input_proj = proj_raw.astype(jnp.float32)
    readout = read_raw.astype(jnp.float32)
    length = inputs.shape[0]
    position = jnp.arange(length)
    causal = (position[:, None] >= position[None, :]).astype(jnp.float32)
    strictly = (position[:, None] < position[None, :]).astype(jnp.float32)
    cumulative = jnp.cumsum(-decay_rate[None] * step_size, axis=0)
    totals = cumulative[-1]
    spread = cumulative[:, None] - cumulative[None, :]
    decays = jnp.exp(jnp.minimum(spread, 0.0)) * causal[:, :, None, None]
    to_end = jnp.exp(totals[None] - cumulative)
    from_start = jnp.exp(cumulative)
    state_match = jnp.einsum("ugn,sgn->usg", read_raw, proj_raw, preferred_element_type=jnp.float32)
    grad_match = jnp.einsum(
        "ughp,sghp->usgh", out_raw, inputs_raw, preferred_element_type=jnp.float32
    )
    mix_input = decays * state_match[..., None]
    back_b = jnp.einsum("ghnp,sgn->sghp", grad_in, input_proj, precision=precise)
    vector = (
        jnp.einsum("usgh,ughp->sghp", mix_input, out_grad, precision=precise)
        + to_end[..., None] * back_b
    )
    grad_inputs = step_size[..., None] * vector
    direct = jnp.sum(inputs * vector, axis=-1)
    mix_state = decays * grad_match * step_size[None]
    back_x = jnp.einsum("ghnp,sghp->sghn", grad_in, inputs, precision=precise)
    grad_proj = jnp.einsum("usgh,ugn->sgn", mix_state, readout, precision=precise) + jnp.einsum(
        "sgh,sghn->sgn", step_size * to_end, back_x, precision=precise
    )
    state_out = jnp.einsum("ghnp,ughp->ughn", state_in, out_grad, precision=precise)
    grad_read = jnp.einsum("usgh,sgn->ugn", mix_state, input_proj, precision=precise) + jnp.einsum(
        "ugh,ughn->ugn", from_start, state_out, precision=precise
    )
    weights = mix_state * state_match[..., None]
    exclusive = jnp.cumsum(weights, axis=1) - weights
    paired = jnp.sum(exclusive * causal[:, :, None, None], axis=0)
    from_init = from_start * jnp.einsum("ugn,ughn->ugh", readout, state_out, precision=precise)
    suffixes = jnp.einsum("ut,ugh->tgh", causal, from_init, precision=precise)
    from_tail = to_end * step_size * jnp.sum(inputs * back_b, axis=-1)
    prefixes = jnp.einsum("st,sgh->tgh", strictly, from_tail, precision=precise)
    constant = jnp.exp(totals) * jnp.sum(grad_in * state_in, axis=(2, 3))
    grad_log = paired + suffixes + prefixes + constant[None]
    grad_step = direct - decay_rate[None] * grad_log
    return (grad_inputs, grad_proj, grad_read, grad_step)


def combine(earlier, later):
    return (earlier[0] + later[0], jnp.exp(later[0])[..., None, None] * earlier[1] + later[1])


def span_prefix(log_sums, states, reverse):
    initial = (jnp.zeros_like(log_sums[0]), jnp.zeros_like(states[0]))

    def advance(carried, element):
        return (combine(carried, element), carried)

    return lax.scan(advance, initial, (log_sums, states), reverse=reverse)


def to_spans(
    inputs, out_grad, input_proj, readout, step_size, group_count, state_dim, head_dim, span_len
):
    span_count = inputs.shape[0] // span_len
    head_count = step_size.shape[1] // group_count
    return (
        inputs.reshape(span_count, span_len, group_count, head_count, head_dim),
        out_grad.reshape(span_count, span_len, group_count, head_count, head_dim),
        input_proj.reshape(span_count, span_len, group_count, state_dim),
        readout.reshape(span_count, span_len, group_count, state_dim),
        step_size.reshape(span_count, span_len, group_count, head_count),
    )


def summaries(blocks, rate_rows):

    def summarize_one(element):
        return summarize(element[0], element[1], element[2], element[3], element[4], rate_rows)

    return lax.map(summarize_one, blocks)


def apply_backward(blocks, rate_rows, state_ins, grad_ins):

    def backward_one(element):
        return span_backward(
            element[0],
            element[1],
            element[2],
            element[3],
            element[4],
            rate_rows,
            element[5],
            element[6],
        )

    gradients = lax.map(backward_one, blocks + (state_ins, grad_ins))
    tokens = gradients[0].shape[0] * gradients[0].shape[1]
    return tuple((item_grad.reshape(tokens, -1) for item_grad in gradients))


def body(inputs, input_proj, readout, step_size, decay_rate, out_grad):
    group_count = input_proj.shape[1] // D_STATE
    blocks = to_spans(
        inputs, out_grad, input_proj, readout, step_size, group_count, D_STATE, HEAD_DIM, SPAN
    )
    rate_rows = decay_rate.reshape(group_count, -1)
    totals, forward, backward = summaries(blocks, rate_rows)
    (device_log, device_fwd), (log_before, fwd_before) = span_prefix(totals, forward, False)
    (ignored_log, device_bwd), (log_after, bwd_after) = span_prefix(totals, backward, True)
    device_in, device_out = seq_scan(device_log, device_fwd, device_bwd, "seq")
    state_ins = fwd_before + jnp.exp(log_before)[..., None, None] * device_in[None]
    grad_ins = bwd_after + jnp.exp(log_after)[..., None, None] * device_out[None]
    grad_inputs, grad_proj, grad_read, grad_step = apply_backward(
        blocks, rate_rows, state_ins, grad_ins
    )
    regrouped = lax.all_to_all(grad_step, "tp", split_axis=0, concat_axis=1, tiled=True)
    return (
        grad_inputs.astype(jnp.bfloat16),
        grad_proj.astype(jnp.bfloat16),
        grad_read.astype(jnp.bfloat16),
        regrouped,
    )


def solution(mesh):
    in_specs = (
        P("seq", "tp"),
        P("seq", "tp"),
        P("seq", "tp"),
        P("seq", "tp"),
        P("tp"),
        P("seq", "tp"),
    )
    out_specs = (P("seq", "tp"), P("seq", "tp"), P("seq", "tp"), P(("seq", "tp"), None))
    return jax.shard_map(body, mesh=mesh, in_specs=in_specs, out_specs=out_specs, check_vma=False)
```

```python
import jax
import numpy as np
import jax.numpy as jnp
from jax import lax
from jax.sharding import PartitionSpec as P

HEAD_DIM = 64
D_STATE = 256
SPAN = 128


precise = lax.Precision.HIGHEST


def prefix(part, axis, combine, identity, reverse):
    count = lax.axis_size(axis)
    place = lax.axis_index(axis)
    ahead = count - 1 - place if reverse else place
    gathered = jax.tree.map(lambda a: lax.all_gather(a, axis), part)
    state = jax.tree.map(lambda a, e: jnp.zeros_like(a) + jnp.asarray(e, a.dtype), part, identity)

    def one(turn, state):
        source = count - 1 - turn if reverse else turn
        return combine(
            state, jax.tree.map(lambda a: lax.dynamic_index_in_dim(a, source, 0, False), gathered)
        )

    return lax.fori_loop(0, ahead, one, state)


def seq_scan(device_log, device_fwd, device_bwd, axis):
    count = lax.axis_size(axis)
    place = lax.axis_index(axis)
    logs = device_log.reshape(-1)
    heads = logs.shape[0]
    stacked = jnp.stack([device_fwd, device_bwd])
    shape = stacked.shape
    combos = 2 * heads
    if combos % count == 0:
        per = combos // count
        targets = np.arange(count)[:, None] * per + np.arange(per)[None, :]
        held = place * per + jnp.arange(per)
    else:
        per = 1
        targets = (np.arange(count) // (count // combos))[:, None]
        held = (place // (count // combos))[None]
    flat = stacked.reshape(count, per, -1)
    tags = jnp.broadcast_to(logs[targets % heads][..., None], (count, per, 128))
    payload = jnp.concatenate([flat, tags], axis=2)
    pieces = lax.all_to_all(payload, axis, 0, 0, tiled=True)
    chosen = pieces[:, :, flat.shape[2]]
    pieces = pieces[:, :, : flat.shape[2]]
    position = jnp.arange(count)
    low = jnp.minimum(position[:, None], position[None, :])
    high = jnp.maximum(position[:, None], position[None, :])
    between = ((position[None, None, :] > low[..., None]) & (position[None, None, :] < high[..., None]))
    exponent = jnp.einsum("ijm,mc->cij", between.astype(jnp.float32), chosen, precision=precise)
    before = (position[None, :] < position[:, None])
    after = (position[None, :] > position[:, None])
    mask = jnp.where((held < heads)[:, None, None], before[None], after[None])
    weights = jnp.where(mask, jnp.exp(exponent), 0.0)
    scanned = jnp.einsum("cij,jcx->icx", weights, pieces, precision=precise)
    back = lax.all_to_all(scanned, axis, 0, 0, tiled=True)
    back = back.reshape(shape)
    return back[0], back[1]

def summarize(inputs, out_grad, input_proj, readout, step_size, decay_rate):
    cumulative = jnp.cumsum(-decay_rate[None] * step_size, axis=0)
    totals = cumulative[-1]
    to_end = jnp.exp(totals[None] - cumulative) * step_size
    forward = jnp.einsum(
        "qghp,qgn->ghnp",
        inputs.astype(jnp.float32) * to_end[..., None],
        input_proj.astype(jnp.float32),
        precision=precise,
    )
    from_start = jnp.exp(cumulative)
    backward = jnp.einsum(
        "qghp,qgn->ghnp",
        out_grad.astype(jnp.float32) * from_start[..., None],
        readout.astype(jnp.float32),
        precision=precise,
    )
    return (totals, forward, backward)


def span_backward(
    inputs_raw, out_raw, proj_raw, read_raw, step_size, decay_rate, state_in, grad_in
):
    inputs = inputs_raw.astype(jnp.float32)
    out_grad = out_raw.astype(jnp.float32)
    input_proj = proj_raw.astype(jnp.float32)
    readout = read_raw.astype(jnp.float32)
    length = inputs.shape[0]
    position = jnp.arange(length)
    causal = (position[:, None] >= position[None, :]).astype(jnp.float32)
    strictly = (position[:, None] < position[None, :]).astype(jnp.float32)
    cumulative = jnp.cumsum(-decay_rate[None] * step_size, axis=0)
    totals = cumulative[-1]
    spread = cumulative[:, None] - cumulative[None, :]
    decays = jnp.exp(jnp.minimum(spread, 0.0)) * causal[:, :, None, None]
    to_end = jnp.exp(totals[None] - cumulative)
    from_start = jnp.exp(cumulative)
    state_match = jnp.einsum("ugn,sgn->usg", read_raw, proj_raw, preferred_element_type=jnp.float32)
    grad_match = jnp.einsum(
        "ughp,sghp->usgh", out_raw, inputs_raw, preferred_element_type=jnp.float32
    )
    mix_input = decays * state_match[..., None]
    back_b = jnp.einsum("ghnp,sgn->sghp", grad_in, input_proj, precision=precise)
    vector = (
        jnp.einsum("usgh,ughp->sghp", mix_input, out_grad, precision=precise)
        + to_end[..., None] * back_b
    )
    grad_inputs = step_size[..., None] * vector
    direct = jnp.sum(inputs * vector, axis=-1)
    mix_state = decays * grad_match * step_size[None]
    back_x = jnp.einsum("ghnp,sghp->sghn", grad_in, inputs, precision=precise)
    grad_proj = jnp.einsum("usgh,ugn->sgn", mix_state, readout, precision=precise) + jnp.einsum(
        "sgh,sghn->sgn", step_size * to_end, back_x, precision=precise
    )
    state_out = jnp.einsum("ghnp,ughp->ughn", state_in, out_grad, precision=precise)
    grad_read = jnp.einsum("usgh,sgn->ugn", mix_state, input_proj, precision=precise) + jnp.einsum(
        "ugh,ughn->ugn", from_start, state_out, precision=precise
    )
    weights = mix_state * state_match[..., None]
    exclusive = jnp.cumsum(weights, axis=1) - weights
    paired = jnp.sum(exclusive * causal[:, :, None, None], axis=0)
    from_init = from_start * jnp.einsum("ugn,ughn->ugh", readout, state_out, precision=precise)
    suffixes = jnp.einsum("ut,ugh->tgh", causal, from_init, precision=precise)
    from_tail = to_end * step_size * jnp.sum(inputs * back_b, axis=-1)
    prefixes = jnp.einsum("st,sgh->tgh", strictly, from_tail, precision=precise)
    constant = jnp.exp(totals) * jnp.sum(grad_in * state_in, axis=(2, 3))
    grad_log = paired + suffixes + prefixes + constant[None]
    grad_step = direct - decay_rate[None] * grad_log
    return (grad_inputs, grad_proj, grad_read, grad_step)


def combine(earlier, later):
    return (earlier[0] + later[0], jnp.exp(later[0])[..., None, None] * earlier[1] + later[1])


def span_prefix(log_sums, states, reverse):
    initial = (jnp.zeros_like(log_sums[0]), jnp.zeros_like(states[0]))

    def advance(carried, element):
        return (combine(carried, element), carried)

    return lax.scan(advance, initial, (log_sums, states), reverse=reverse)


def to_spans(
    inputs, out_grad, input_proj, readout, step_size, group_count, state_dim, head_dim, span_len
):
    span_count = inputs.shape[0] // span_len
    head_count = step_size.shape[1] // group_count
    return (
        inputs.reshape(span_count, span_len, group_count, head_count, head_dim),
        out_grad.reshape(span_count, span_len, group_count, head_count, head_dim),
        input_proj.reshape(span_count, span_len, group_count, state_dim),
        readout.reshape(span_count, span_len, group_count, state_dim),
        step_size.reshape(span_count, span_len, group_count, head_count),
    )


def summaries(blocks, rate_rows):

    def summarize_one(element):
        return summarize(element[0], element[1], element[2], element[3], element[4], rate_rows)

    return lax.map(summarize_one, blocks)


def apply_backward(blocks, rate_rows, state_ins, grad_ins):

    def backward_one(element):
        return span_backward(
            element[0],
            element[1],
            element[2],
            element[3],
            element[4],
            rate_rows,
            element[5],
            element[6],
        )

    gradients = lax.map(backward_one, blocks + (state_ins, grad_ins))
    tokens = gradients[0].shape[0] * gradients[0].shape[1]
    return tuple((item_grad.reshape(tokens, -1) for item_grad in gradients))


def body(inputs, input_proj, readout, step_size, decay_rate, out_grad):
    group_count = input_proj.shape[1] // D_STATE
    blocks = to_spans(
        inputs, out_grad, input_proj, readout, step_size, group_count, D_STATE, HEAD_DIM, SPAN
    )
    rate_rows = decay_rate.reshape(group_count, -1)
    totals, forward, backward = summaries(blocks, rate_rows)
    (device_log, device_fwd), (log_before, fwd_before) = span_prefix(totals, forward, False)
    (ignored_log, device_bwd), (log_after, bwd_after) = span_prefix(totals, backward, True)
    device_in, device_out = seq_scan(device_log, device_fwd, device_bwd, "seq")
    state_ins = fwd_before + jnp.exp(log_before)[..., None, None] * device_in[None]
    grad_ins = bwd_after + jnp.exp(log_after)[..., None, None] * device_out[None]
    grad_inputs, grad_proj, grad_read, grad_step = apply_backward(
        blocks, rate_rows, state_ins, grad_ins
    )
    regrouped = lax.all_to_all(grad_step, "tp", split_axis=0, concat_axis=1, tiled=True)
    return (
        grad_inputs.astype(jnp.bfloat16),
        grad_proj.astype(jnp.bfloat16),
        grad_read.astype(jnp.bfloat16),
        regrouped,
    )


def solution(mesh):
    in_specs = (
        P("seq", "tp"),
        P("seq", "tp"),
        P("seq", "tp"),
        P("seq", "tp"),
        P("tp"),
        P("seq", "tp"),
    )
    out_specs = (P("seq", "tp"), P("seq", "tp"), P("seq", "tp"), P(("seq", "tp"), None))
    return jax.shard_map(body, mesh=mesh, in_specs=in_specs, out_specs=out_specs, check_vma=False)
```

```python
import jax
import numpy as np
import jax.numpy as jnp
from jax import lax
from jax.sharding import PartitionSpec as P

HEAD_DIM = 64
D_STATE = 256
SPAN = 128


precise = lax.Precision.HIGHEST


def prefix(part, axis, combine, identity, reverse):
    count = lax.axis_size(axis)
    place = lax.axis_index(axis)
    ahead = count - 1 - place if reverse else place
    gathered = jax.tree.map(lambda a: lax.all_gather(a, axis), part)
    state = jax.tree.map(lambda a, e: jnp.zeros_like(a) + jnp.asarray(e, a.dtype), part, identity)

    def one(turn, state):
        source = count - 1 - turn if reverse else turn
        return combine(
            state, jax.tree.map(lambda a: lax.dynamic_index_in_dim(a, source, 0, False), gathered)
        )

    return lax.fori_loop(0, ahead, one, state)


def seq_scan(device_log, device_fwd, device_bwd, axis):
    count = lax.axis_size(axis)
    place = lax.axis_index(axis)
    logs = device_log.reshape(-1)
    heads = logs.shape[0]
    stacked = jnp.stack([device_fwd, device_bwd]).transpose(0, 1, 3, 2, 4)
    shape = stacked.shape
    combos = 2 * heads
    if combos % count == 0:
        per = combos // count
        targets = np.arange(count)[:, None] * per + np.arange(per)[None, :]
        held = place * per + jnp.arange(per)
    else:
        per = 1
        targets = (np.arange(count) // (count // combos))[:, None]
        held = (place // (count // combos))[None]
    flat = stacked.reshape(count, per, -1)
    tags = jnp.broadcast_to(logs[targets % heads][..., None], (count, per, 128))
    payload = jnp.concatenate([flat, tags], axis=2)
    pieces = lax.all_to_all(payload, axis, 0, 0, tiled=True)
    chosen = pieces[:, :, flat.shape[2]]
    pieces = pieces[:, :, : flat.shape[2]]
    position = jnp.arange(count)
    low = jnp.minimum(position[:, None], position[None, :])
    high = jnp.maximum(position[:, None], position[None, :])
    between = ((position[None, None, :] > low[..., None]) & (position[None, None, :] < high[..., None]))
    exponent = jnp.einsum("ijm,mc->cij", between.astype(jnp.float32), chosen, precision=precise)
    before = (position[None, :] < position[:, None])
    after = (position[None, :] > position[:, None])
    mask = jnp.where((held < heads)[:, None, None], before[None], after[None])
    weights = jnp.where(mask, jnp.exp(exponent), 0.0)
    scanned = jnp.einsum("cij,jcx->icx", weights, pieces, precision=precise)
    back = lax.all_to_all(scanned, axis, 0, 0, tiled=True)
    back = back.reshape(shape).transpose(0, 1, 3, 2, 4)
    return back[0], back[1]

def summarize(inputs, out_grad, input_proj, readout, step_size, decay_rate):
    cumulative = jnp.cumsum(-decay_rate[None] * step_size, axis=0)
    totals = cumulative[-1]
    to_end = jnp.exp(totals[None] - cumulative) * step_size
    forward = jnp.einsum(
        "qghp,qgn->gnhp",
        inputs.astype(jnp.float32) * to_end[..., None],
        input_proj.astype(jnp.float32),
        precision=precise,
    )
    from_start = jnp.exp(cumulative)
    backward = jnp.einsum(
        "qghp,qgn->gnhp",
        out_grad.astype(jnp.float32) * from_start[..., None],
        readout.astype(jnp.float32),
        precision=precise,
    )
    return (totals, forward, backward)


def span_local(inputs_raw, out_raw, proj_raw, read_raw, step_size, decay_rate):
    inputs = inputs_raw.astype(jnp.float32)
    out_grad = out_raw.astype(jnp.float32)
    input_proj = proj_raw.astype(jnp.float32)
    readout = read_raw.astype(jnp.float32)
    length = inputs.shape[0]
    position = jnp.arange(length)
    causal = (position[:, None] >= position[None, :]).astype(jnp.float32)
    cumulative = jnp.cumsum(-decay_rate[None] * step_size, axis=0)
    totals = cumulative[-1]
    spread = cumulative[:, None] - cumulative[None, :]
    decays = jnp.exp(jnp.minimum(spread, 0.0)) * causal[:, :, None, None]
    to_end = jnp.exp(totals[None] - cumulative)
    from_start = jnp.exp(cumulative)
    state_match = jnp.einsum("ugn,sgn->usg", read_raw, proj_raw, preferred_element_type=jnp.float32)
    grad_match = jnp.einsum(
        "ughp,sghp->usgh", out_raw, inputs_raw, preferred_element_type=jnp.float32
    )
    mix_input = decays * state_match[..., None]
    vector = jnp.einsum("usgh,ughp->sghp", mix_input, out_grad, precision=precise)
    direct = jnp.sum(inputs * vector, axis=-1)
    mix_state = decays * grad_match * step_size[None]
    grad_proj = jnp.einsum("usgh,ugn->sgn", mix_state, readout, precision=precise)
    grad_read = jnp.einsum("usgh,sgn->ugn", mix_state, input_proj, precision=precise)
    weights = mix_state * state_match[..., None]
    exclusive = jnp.cumsum(weights, axis=1) - weights
    paired = jnp.sum(exclusive * causal[:, :, None, None], axis=0)
    return (vector, direct, grad_proj, grad_read, paired)


def span_state(
    inputs_raw, out_raw, proj_raw, read_raw, step_size, decay_rate, state_in, grad_in, local
):
    vector, direct, grad_proj, grad_read, paired = local
    inputs = inputs_raw.astype(jnp.float32)
    out_grad = out_raw.astype(jnp.float32)
    input_proj = proj_raw.astype(jnp.float32)
    readout = read_raw.astype(jnp.float32)
    length = inputs.shape[0]
    position = jnp.arange(length)
    causal = (position[:, None] >= position[None, :]).astype(jnp.float32)
    strictly = (position[:, None] < position[None, :]).astype(jnp.float32)
    cumulative = jnp.cumsum(-decay_rate[None] * step_size, axis=0)
    totals = cumulative[-1]
    to_end = jnp.exp(totals[None] - cumulative)
    from_start = jnp.exp(cumulative)
    back_b = jnp.einsum("gnhp,sgn->sghp", grad_in, input_proj, precision=precise)
    vector = vector + to_end[..., None] * back_b
    grad_inputs = step_size[..., None] * vector
    tail_dot = jnp.sum(inputs * back_b, axis=-1)
    direct = direct + to_end * tail_dot
    scaled_x = (step_size * to_end)[..., None] * inputs
    grad_proj = grad_proj + jnp.einsum("sghp,gnhp->sgn", scaled_x, grad_in, precision=precise)
    scaled_y = from_start[..., None] * out_grad
    grad_read = grad_read + jnp.einsum("ughp,gnhp->ugn", scaled_y, state_in, precision=precise)
    read_state = jnp.einsum("ugn,gnhp->ughp", readout, state_in, precision=precise)
    from_init = from_start * jnp.sum(read_state * out_grad, axis=-1)
    suffixes = jnp.einsum("ut,ugh->tgh", causal, from_init, precision=precise)
    from_tail = to_end * step_size * tail_dot
    prefixes = jnp.einsum("st,sgh->tgh", strictly, from_tail, precision=precise)
    constant = jnp.exp(totals) * jnp.einsum("gnhp,gnhp->gh", grad_in, state_in, precision=precise)
    grad_log = paired + suffixes + prefixes + constant[None]
    grad_step = direct - decay_rate[None] * grad_log
    return (grad_inputs, grad_proj, grad_read, grad_step)


def combine(earlier, later):
    return (earlier[0] + later[0], jnp.exp(later[0])[:, None, :, None] * earlier[1] + later[1])


def span_prefix(log_sums, states, reverse):
    initial = (jnp.zeros_like(log_sums[0]), jnp.zeros_like(states[0]))

    def advance(carried, element):
        return (combine(carried, element), carried)

    return lax.scan(advance, initial, (log_sums, states), reverse=reverse)


def to_spans(
    inputs, out_grad, input_proj, readout, step_size, group_count, state_dim, head_dim, span_len
):
    span_count = inputs.shape[0] // span_len
    head_count = step_size.shape[1] // group_count
    return (
        inputs.reshape(span_count, span_len, group_count, head_count, head_dim),
        out_grad.reshape(span_count, span_len, group_count, head_count, head_dim),
        input_proj.reshape(span_count, span_len, group_count, state_dim),
        readout.reshape(span_count, span_len, group_count, state_dim),
        step_size.reshape(span_count, span_len, group_count, head_count),
    )


def over_spans(function, items):
    if jax.tree.leaves(items)[0].shape[0] == 1:
        return jax.tree.map(lambda a: a[None], function(jax.tree.map(lambda a: a[0], items)))
    return lax.map(function, items)


def body(inputs, input_proj, readout, step_size, decay_rate, out_grad):
    group_count = input_proj.shape[1] // D_STATE
    blocks = to_spans(
        inputs, out_grad, input_proj, readout, step_size, group_count, D_STATE, HEAD_DIM, SPAN
    )
    rate_rows = decay_rate.reshape(group_count, -1)
    totals, forward, backward = over_spans(lambda e: summarize(*e, rate_rows), blocks)
    if totals.shape[0] == 1:
        device_log, device_fwd, device_bwd = totals[0], forward[0], backward[0]
        log_before = log_after = jnp.zeros_like(totals)
        fwd_before = bwd_after = jnp.zeros_like(forward)
    else:
        (device_log, device_fwd), (log_before, fwd_before) = span_prefix(totals, forward, False)
        (ignored_log, device_bwd), (log_after, bwd_after) = span_prefix(totals, backward, True)
    local = over_spans(lambda e: span_local(*e, rate_rows), blocks)
    device_in, device_out = seq_scan(device_log, device_fwd, device_bwd, "seq")
    state_ins = fwd_before + jnp.exp(log_before)[:, :, None, :, None] * device_in[None]
    grad_ins = bwd_after + jnp.exp(log_after)[:, :, None, :, None] * device_out[None]
    gradients = over_spans(
        lambda e: span_state(*e[0], rate_rows, e[1], e[2], e[3]),
        (blocks, state_ins, grad_ins, local),
    )
    tokens = gradients[0].shape[0] * gradients[0].shape[1]
    grad_inputs, grad_proj, grad_read, grad_step = (g.reshape(tokens, -1) for g in gradients)
    regrouped = lax.all_to_all(grad_step, "tp", split_axis=0, concat_axis=1, tiled=True)
    return (
        grad_inputs.astype(jnp.bfloat16),
        grad_proj.astype(jnp.bfloat16),
        grad_read.astype(jnp.bfloat16),
        regrouped,
    )


def solution(mesh):
    in_specs = (
        P("seq", "tp"),
        P("seq", "tp"),
        P("seq", "tp"),
        P("seq", "tp"),
        P("tp"),
        P("seq", "tp"),
    )
    out_specs = (P("seq", "tp"), P("seq", "tp"), P("seq", "tp"), P(("seq", "tp"), None))
    return jax.shard_map(body, mesh=mesh, in_specs=in_specs, out_specs=out_specs, check_vma=False)
```

```python
import jax
import numpy as np
import jax.numpy as jnp
from jax import lax
from jax.sharding import PartitionSpec as P

HEAD_DIM = 64
D_STATE = 256
SPAN = 128


precise = lax.Precision.HIGHEST


def prefix(part, axis, combine, identity, reverse):
    count = lax.axis_size(axis)
    place = lax.axis_index(axis)
    ahead = count - 1 - place if reverse else place
    gathered = jax.tree.map(lambda a: lax.all_gather(a, axis), part)
    state = jax.tree.map(lambda a, e: jnp.zeros_like(a) + jnp.asarray(e, a.dtype), part, identity)

    def one(turn, state):
        source = count - 1 - turn if reverse else turn
        return combine(
            state, jax.tree.map(lambda a: lax.dynamic_index_in_dim(a, source, 0, False), gathered)
        )

    return lax.fori_loop(0, ahead, one, state)


def seq_scan(device_log, device_fwd, device_bwd, axis):
    count = lax.axis_size(axis)
    place = lax.axis_index(axis)
    logs = device_log.reshape(-1)
    heads = logs.shape[0]
    stacked = jnp.stack([device_fwd, device_bwd]).transpose(0, 1, 3, 2, 4)
    shape = stacked.shape
    combos = 2 * heads
    if combos % count == 0:
        per = combos // count
        targets = np.arange(count)[:, None] * per + np.arange(per)[None, :]
        held = place * per + jnp.arange(per)
    else:
        per = 1
        targets = (np.arange(count) // (count // combos))[:, None]
        held = (place // (count // combos))[None]
    flat = stacked.reshape(count, per * 8, -1)
    width = flat.shape[2]
    tags = jnp.repeat(logs[targets % heads], 8, axis=1)
    tags = jnp.broadcast_to(tags[..., None], (count, per * 8, 128))
    payload = jnp.concatenate([flat, tags], axis=2)
    pieces = lax.all_to_all(payload, axis, 0, 0, tiled=True)
    chosen = pieces[:, ::8, width]
    pieces = pieces[:, :, :width].reshape(count, per, -1)
    position = jnp.arange(count)
    low = jnp.minimum(position[:, None], position[None, :])
    high = jnp.maximum(position[:, None], position[None, :])
    between = ((position[None, None, :] > low[..., None]) & (position[None, None, :] < high[..., None]))
    exponent = jnp.einsum("ijm,mc->cij", between.astype(jnp.float32), chosen, precision=precise)
    before = (position[None, :] < position[:, None])
    after = (position[None, :] > position[:, None])
    mask = jnp.where((held < heads)[:, None, None], before[None], after[None])
    weights = jnp.where(mask, jnp.exp(exponent), 0.0)
    scanned = jnp.einsum("cij,jcx->icx", weights, pieces, precision=precise)
    back = lax.all_to_all(scanned.reshape(count, per * 8, -1), axis, 0, 0, tiled=True)
    back = back.reshape(shape).transpose(0, 1, 3, 2, 4)
    return back[0], back[1]

def summarize(inputs, out_grad, input_proj, readout, step_size, decay_rate):
    cumulative = jnp.cumsum(-decay_rate[None] * step_size, axis=0)
    totals = cumulative[-1]
    to_end = jnp.exp(totals[None] - cumulative) * step_size
    forward = jnp.einsum(
        "qghp,qgn->gnhp",
        inputs.astype(jnp.float32) * to_end[..., None],
        input_proj.astype(jnp.float32),
        precision=precise,
    )
    from_start = jnp.exp(cumulative)
    backward = jnp.einsum(
        "qghp,qgn->gnhp",
        out_grad.astype(jnp.float32) * from_start[..., None],
        readout.astype(jnp.float32),
        precision=precise,
    )
    return (totals, forward, backward)


def span_local(inputs_raw, out_raw, proj_raw, read_raw, step_size, decay_rate):
    inputs = inputs_raw.astype(jnp.float32)
    out_grad = out_raw.astype(jnp.float32)
    input_proj = proj_raw.astype(jnp.float32)
    readout = read_raw.astype(jnp.float32)
    length = inputs.shape[0]
    position = jnp.arange(length)
    causal = (position[:, None] >= position[None, :]).astype(jnp.float32)
    cumulative = jnp.cumsum(-decay_rate[None] * step_size, axis=0)
    totals = cumulative[-1]
    spread = cumulative[:, None] - cumulative[None, :]
    decays = jnp.exp(jnp.minimum(spread, 0.0)) * causal[:, :, None, None]
    to_end = jnp.exp(totals[None] - cumulative)
    from_start = jnp.exp(cumulative)
    state_match = jnp.einsum("ugn,sgn->usg", read_raw, proj_raw, preferred_element_type=jnp.float32)
    grad_match = jnp.einsum(
        "ughp,sghp->usgh", out_raw, inputs_raw, preferred_element_type=jnp.float32
    )
    mix_input = decays * state_match[..., None]
    vector = jnp.einsum("usgh,ughp->sghp", mix_input, out_grad, precision=precise)
    direct = jnp.sum(inputs * vector, axis=-1)
    mix_state = decays * grad_match * step_size[None]
    grad_proj = jnp.einsum("usgh,ugn->sgn", mix_state, readout, precision=precise)
    grad_read = jnp.einsum("usgh,sgn->ugn", mix_state, input_proj, precision=precise)
    weights = mix_state * state_match[..., None]
    exclusive = jnp.cumsum(weights, axis=1) - weights
    paired = jnp.sum(exclusive * causal[:, :, None, None], axis=0)
    return (vector, direct, grad_proj, grad_read, paired)


def span_state(
    inputs_raw, out_raw, proj_raw, read_raw, step_size, decay_rate, state_in, grad_in, local
):
    vector, direct, grad_proj, grad_read, paired = local
    inputs = inputs_raw.astype(jnp.float32)
    out_grad = out_raw.astype(jnp.float32)
    input_proj = proj_raw.astype(jnp.float32)
    readout = read_raw.astype(jnp.float32)
    length = inputs.shape[0]
    position = jnp.arange(length)
    causal = (position[:, None] >= position[None, :]).astype(jnp.float32)
    strictly = (position[:, None] < position[None, :]).astype(jnp.float32)
    cumulative = jnp.cumsum(-decay_rate[None] * step_size, axis=0)
    totals = cumulative[-1]
    to_end = jnp.exp(totals[None] - cumulative)
    from_start = jnp.exp(cumulative)
    back_b = jnp.einsum("gnhp,sgn->sghp", grad_in, input_proj, precision=precise)
    vector = vector + to_end[..., None] * back_b
    grad_inputs = step_size[..., None] * vector
    tail_dot = jnp.sum(inputs * back_b, axis=-1)
    direct = direct + to_end * tail_dot
    scaled_x = (step_size * to_end)[..., None] * inputs
    grad_proj = grad_proj + jnp.einsum("sghp,gnhp->sgn", scaled_x, grad_in, precision=precise)
    scaled_y = from_start[..., None] * out_grad
    grad_read = grad_read + jnp.einsum("ughp,gnhp->ugn", scaled_y, state_in, precision=precise)
    read_state = jnp.einsum("ugn,gnhp->ughp", readout, state_in, precision=precise)
    from_init = from_start * jnp.sum(read_state * out_grad, axis=-1)
    suffixes = jnp.einsum("ut,ugh->tgh", causal, from_init, precision=precise)
    from_tail = to_end * step_size * tail_dot
    prefixes = jnp.einsum("st,sgh->tgh", strictly, from_tail, precision=precise)
    constant = jnp.exp(totals) * jnp.einsum("gnhp,gnhp->gh", grad_in, state_in, precision=precise)
    grad_log = paired + suffixes + prefixes + constant[None]
    grad_step = direct - decay_rate[None] * grad_log
    return (grad_inputs, grad_proj, grad_read, grad_step)


def combine(earlier, later):
    return (earlier[0] + later[0], jnp.exp(later[0])[:, None, :, None] * earlier[1] + later[1])


def span_prefix(log_sums, states, reverse):
    initial = (jnp.zeros_like(log_sums[0]), jnp.zeros_like(states[0]))

    def advance(carried, element):
        return (combine(carried, element), carried)

    return lax.scan(advance, initial, (log_sums, states), reverse=reverse)


def to_spans(
    inputs, out_grad, input_proj, readout, step_size, group_count, state_dim, head_dim, span_len
):
    span_count = inputs.shape[0] // span_len
    head_count = step_size.shape[1] // group_count
    return (
        inputs.reshape(span_count, span_len, group_count, head_count, head_dim),
        out_grad.reshape(span_count, span_len, group_count, head_count, head_dim),
        input_proj.reshape(span_count, span_len, group_count, state_dim),
        readout.reshape(span_count, span_len, group_count, state_dim),
        step_size.reshape(span_count, span_len, group_count, head_count),
    )


def over_spans(function, items):
    if jax.tree.leaves(items)[0].shape[0] == 1:
        return jax.tree.map(lambda a: a[None], function(jax.tree.map(lambda a: a[0], items)))
    return lax.map(function, items)


def body(inputs, input_proj, readout, step_size, decay_rate, out_grad):
    group_count = input_proj.shape[1] // D_STATE
    blocks = to_spans(
        inputs, out_grad, input_proj, readout, step_size, group_count, D_STATE, HEAD_DIM, SPAN
    )
    rate_rows = decay_rate.reshape(group_count, -1)
    totals, forward, backward = over_spans(lambda e: summarize(*e, rate_rows), blocks)
    if totals.shape[0] == 1:
        device_log, device_fwd, device_bwd = totals[0], forward[0], backward[0]
        log_before = log_after = jnp.zeros_like(totals)
        fwd_before = bwd_after = jnp.zeros_like(forward)
    else:
        (device_log, device_fwd), (log_before, fwd_before) = span_prefix(totals, forward, False)
        (ignored_log, device_bwd), (log_after, bwd_after) = span_prefix(totals, backward, True)
    local = over_spans(lambda e: span_local(*e, rate_rows), blocks)
    device_in, device_out = seq_scan(device_log, device_fwd, device_bwd, "seq")
    state_ins = fwd_before + jnp.exp(log_before)[:, :, None, :, None] * device_in[None]
    grad_ins = bwd_after + jnp.exp(log_after)[:, :, None, :, None] * device_out[None]
    gradients = over_spans(
        lambda e: span_state(*e[0], rate_rows, e[1], e[2], e[3]),
        (blocks, state_ins, grad_ins, local),
    )
    tokens = gradients[0].shape[0] * gradients[0].shape[1]
    grad_inputs, grad_proj, grad_read, grad_step = (g.reshape(tokens, -1) for g in gradients)
    regrouped = lax.all_to_all(grad_step, "tp", split_axis=0, concat_axis=1, tiled=True)
    return (
        grad_inputs.astype(jnp.bfloat16),
        grad_proj.astype(jnp.bfloat16),
        grad_read.astype(jnp.bfloat16),
        regrouped,
    )


def solution(mesh):
    in_specs = (
        P("seq", "tp"),
        P("seq", "tp"),
        P("seq", "tp"),
        P("seq", "tp"),
        P("tp"),
        P("seq", "tp"),
    )
    out_specs = (P("seq", "tp"), P("seq", "tp"), P("seq", "tp"), P(("seq", "tp"), None))
    return jax.shard_map(body, mesh=mesh, in_specs=in_specs, out_specs=out_specs, check_vma=False)
```

```python
import jax
import numpy as np
import jax.numpy as jnp
from jax import lax
from jax.sharding import Mesh, PartitionSpec as P

HEAD_DIM = 64
D_STATE = 256
SPAN = 128


precise = lax.Precision.HIGHEST


def prefix(part, axis, combine, identity, reverse):
    count = lax.axis_size(axis)
    place = lax.axis_index(axis)
    ahead = count - 1 - place if reverse else place
    gathered = jax.tree.map(lambda a: lax.all_gather(a, axis), part)
    state = jax.tree.map(lambda a, e: jnp.zeros_like(a) + jnp.asarray(e, a.dtype), part, identity)

    def one(turn, state):
        source = count - 1 - turn if reverse else turn
        return combine(
            state, jax.tree.map(lambda a: lax.dynamic_index_in_dim(a, source, 0, False), gathered)
        )

    return lax.fori_loop(0, ahead, one, state)


def spread(values, tags, axis):
    count, per, size = values.shape
    rows = values.reshape(count, per * 8, size // 8)
    tag = jnp.broadcast_to(jnp.repeat(tags, 8, axis=1)[..., None], (count, per * 8, 128))
    got = lax.all_to_all(jnp.concatenate([rows, tag], axis=2), axis, 0, 0, tiled=True)
    return got[:, :, : size // 8].reshape(count, per, size), got[:, ::8, size // 8]


def gather_back(values, axis):
    count, per, size = values.shape
    got = lax.all_to_all(values.reshape(count, per * 8, size // 8), axis, 0, 0, tiled=True)
    return got.reshape(count, per, size)


def scan_weights(logs, forward):
    count = logs.shape[0]
    position = np.arange(count)
    low = np.minimum(position[:, None], position[None, :])
    high = np.maximum(position[:, None], position[None, :])
    between = (position[None, None, :] > low[..., None]) & (position[None, None, :] < high[..., None])
    below = (position[None, :] < position[:, None]).astype(np.float32)
    above = (position[None, :] > position[:, None]).astype(np.float32)
    inner = jnp.einsum("ijm,mc->cij", between.astype(np.float32), logs, precision=precise)
    mask = jnp.where(forward[:, None, None], below[None] > 0, above[None] > 0)
    weights = jnp.where(mask, jnp.exp(inner), 0.0)
    before = jnp.einsum("im,mc->ci", below, logs, precision=precise)
    after = jnp.einsum("im,mc->ci", above, logs, precision=precise)
    total = jnp.exp(jnp.where(forward[:, None], after, before))
    entry = jnp.exp(jnp.where(forward[:, None], before, after))
    return weights, total, entry


def seq_scan(device_log, device_fwd, device_bwd, outer, inner):
    logs = device_log.reshape(-1)
    heads = logs.shape[0]
    stacked = jnp.stack([device_fwd, device_bwd]).transpose(0, 1, 3, 2, 4)
    shape = stacked.shape
    members = lax.axis_size(inner)
    groups = lax.axis_size(outer)
    per = 2 * heads // members
    targets = np.arange(members)[:, None] * per + np.arange(per)[None, :]
    held = lax.axis_index(inner) * per + jnp.arange(per)
    pieces, member_logs = spread(stacked.reshape(members, per, -1), logs[targets % heads], inner)
    weights, total, entry = scan_weights(member_logs, held < heads)
    local = jnp.einsum("cij,jcx->icx", weights, pieces, precision=precise)
    summary = jnp.einsum("cj,jcx->cx", total, pieces, precision=precise)
    group_log = jnp.sum(member_logs, axis=0)
    split = per // groups
    chunks, group_logs = spread(summary.reshape(groups, split, -1), group_log.reshape(groups, split), outer)
    mine = held.reshape(groups, split)[lax.axis_index(outer)]
    group_weights, ignored_total, ignored_entry = scan_weights(group_logs, mine < heads)
    scanned = jnp.einsum("cij,jcx->icx", group_weights, chunks, precision=precise)
    incoming = gather_back(scanned, outer).reshape(per, -1)
    result = local + entry.T[..., None] * incoming[None]
    back = gather_back(result, inner).reshape(shape).transpose(0, 1, 3, 2, 4)
    return back[0], back[1]

def summarize(inputs, out_grad, input_proj, readout, step_size, decay_rate):
    cumulative = jnp.cumsum(-decay_rate[None] * step_size, axis=0)
    totals = cumulative[-1]
    to_end = jnp.exp(totals[None] - cumulative) * step_size
    forward = jnp.einsum(
        "qghp,qgn->gnhp",
        inputs.astype(jnp.float32) * to_end[..., None],
        input_proj.astype(jnp.float32),
        precision=precise,
    )
    from_start = jnp.exp(cumulative)
    backward = jnp.einsum(
        "qghp,qgn->gnhp",
        out_grad.astype(jnp.float32) * from_start[..., None],
        readout.astype(jnp.float32),
        precision=precise,
    )
    return (totals, forward, backward)


def span_local(inputs_raw, out_raw, proj_raw, read_raw, step_size, decay_rate):
    inputs = inputs_raw.astype(jnp.float32)
    out_grad = out_raw.astype(jnp.float32)
    input_proj = proj_raw.astype(jnp.float32)
    readout = read_raw.astype(jnp.float32)
    length = inputs.shape[0]
    position = jnp.arange(length)
    causal = (position[:, None] >= position[None, :]).astype(jnp.float32)
    cumulative = jnp.cumsum(-decay_rate[None] * step_size, axis=0)
    totals = cumulative[-1]
    spread = cumulative[:, None] - cumulative[None, :]
    decays = jnp.exp(jnp.minimum(spread, 0.0)) * causal[:, :, None, None]
    to_end = jnp.exp(totals[None] - cumulative)
    from_start = jnp.exp(cumulative)
    state_match = jnp.einsum("ugn,sgn->usg", read_raw, proj_raw, preferred_element_type=jnp.float32)
    grad_match = jnp.einsum(
        "ughp,sghp->usgh", out_raw, inputs_raw, preferred_element_type=jnp.float32
    )
    mix_input = decays * state_match[..., None]
    vector = jnp.einsum("usgh,ughp->sghp", mix_input, out_grad, precision=precise)
    direct = jnp.sum(inputs * vector, axis=-1)
    mix_state = decays * grad_match * step_size[None]
    grad_proj = jnp.einsum("usgh,ugn->sgn", mix_state, readout, precision=precise)
    grad_read = jnp.einsum("usgh,sgn->ugn", mix_state, input_proj, precision=precise)
    weights = mix_state * state_match[..., None]
    exclusive = jnp.cumsum(weights, axis=1) - weights
    paired = jnp.sum(exclusive * causal[:, :, None, None], axis=0)
    return (vector, direct, grad_proj, grad_read, paired)


def span_state(
    inputs_raw, out_raw, proj_raw, read_raw, step_size, decay_rate, state_in, grad_in, local
):
    vector, direct, grad_proj, grad_read, paired = local
    inputs = inputs_raw.astype(jnp.float32)
    out_grad = out_raw.astype(jnp.float32)
    input_proj = proj_raw.astype(jnp.float32)
    readout = read_raw.astype(jnp.float32)
    length = inputs.shape[0]
    position = jnp.arange(length)
    causal = (position[:, None] >= position[None, :]).astype(jnp.float32)
    strictly = (position[:, None] < position[None, :]).astype(jnp.float32)
    cumulative = jnp.cumsum(-decay_rate[None] * step_size, axis=0)
    totals = cumulative[-1]
    to_end = jnp.exp(totals[None] - cumulative)
    from_start = jnp.exp(cumulative)
    back_b = jnp.einsum("gnhp,sgn->sghp", grad_in, input_proj, precision=precise)
    vector = vector + to_end[..., None] * back_b
    grad_inputs = step_size[..., None] * vector
    tail_dot = jnp.sum(inputs * back_b, axis=-1)
    direct = direct + to_end * tail_dot
    scaled_x = (step_size * to_end)[..., None] * inputs
    grad_proj = grad_proj + jnp.einsum("sghp,gnhp->sgn", scaled_x, grad_in, precision=precise)
    scaled_y = from_start[..., None] * out_grad
    grad_read = grad_read + jnp.einsum("ughp,gnhp->ugn", scaled_y, state_in, precision=precise)
    read_state = jnp.einsum("ugn,gnhp->ughp", readout, state_in, precision=precise)
    from_init = from_start * jnp.sum(read_state * out_grad, axis=-1)
    suffixes = jnp.einsum("ut,ugh->tgh", causal, from_init, precision=precise)
    from_tail = to_end * step_size * tail_dot
    prefixes = jnp.einsum("st,sgh->tgh", strictly, from_tail, precision=precise)
    constant = jnp.exp(totals) * jnp.einsum("gnhp,gnhp->gh", grad_in, state_in, precision=precise)
    grad_log = paired + suffixes + prefixes + constant[None]
    grad_step = direct - decay_rate[None] * grad_log
    return (grad_inputs, grad_proj, grad_read, grad_step)


def combine(earlier, later):
    return (earlier[0] + later[0], jnp.exp(later[0])[:, None, :, None] * earlier[1] + later[1])


def span_prefix(log_sums, states, reverse):
    initial = (jnp.zeros_like(log_sums[0]), jnp.zeros_like(states[0]))

    def advance(carried, element):
        return (combine(carried, element), carried)

    return lax.scan(advance, initial, (log_sums, states), reverse=reverse)


def to_spans(
    inputs, out_grad, input_proj, readout, step_size, group_count, state_dim, head_dim, span_len
):
    span_count = inputs.shape[0] // span_len
    head_count = step_size.shape[1] // group_count
    return (
        inputs.reshape(span_count, span_len, group_count, head_count, head_dim),
        out_grad.reshape(span_count, span_len, group_count, head_count, head_dim),
        input_proj.reshape(span_count, span_len, group_count, state_dim),
        readout.reshape(span_count, span_len, group_count, state_dim),
        step_size.reshape(span_count, span_len, group_count, head_count),
    )


def over_spans(function, items):
    if jax.tree.leaves(items)[0].shape[0] == 1:
        return jax.tree.map(lambda a: a[None], function(jax.tree.map(lambda a: a[0], items)))
    return lax.map(function, items)


def body(inputs, input_proj, readout, step_size, decay_rate, out_grad):
    group_count = input_proj.shape[1] // D_STATE
    blocks = to_spans(
        inputs, out_grad, input_proj, readout, step_size, group_count, D_STATE, HEAD_DIM, SPAN
    )
    rate_rows = decay_rate.reshape(group_count, -1)
    totals, forward, backward = over_spans(lambda e: summarize(*e, rate_rows), blocks)
    if totals.shape[0] == 1:
        device_log, device_fwd, device_bwd = totals[0], forward[0], backward[0]
        log_before = log_after = jnp.zeros_like(totals)
        fwd_before = bwd_after = jnp.zeros_like(forward)
    else:
        (device_log, device_fwd), (log_before, fwd_before) = span_prefix(totals, forward, False)
        (ignored_log, device_bwd), (log_after, bwd_after) = span_prefix(totals, backward, True)
    local = over_spans(lambda e: span_local(*e, rate_rows), blocks)
    device_in, device_out = seq_scan(device_log, device_fwd, device_bwd, "z", "x")
    state_ins = fwd_before + jnp.exp(log_before)[:, :, None, :, None] * device_in[None]
    grad_ins = bwd_after + jnp.exp(log_after)[:, :, None, :, None] * device_out[None]
    gradients = over_spans(
        lambda e: span_state(*e[0], rate_rows, e[1], e[2], e[3]),
        (blocks, state_ins, grad_ins, local),
    )
    tokens = gradients[0].shape[0] * gradients[0].shape[1]
    grad_inputs, grad_proj, grad_read, grad_step = (g.reshape(tokens, -1) for g in gradients)
    regrouped = lax.all_to_all(grad_step, "tp", split_axis=0, concat_axis=1, tiled=True)
    return (
        grad_inputs.astype(jnp.bfloat16),
        grad_proj.astype(jnp.bfloat16),
        grad_read.astype(jnp.bfloat16),
        regrouped,
    )


def solution(mesh):
    rows = mesh.devices.shape[0]
    inner = len({device.coords[0] for device in mesh.devices[:, 0]})
    grid = Mesh(mesh.devices.reshape(rows // inner, inner, -1), ("z", "x", "tp"))
    seq = ("z", "x")
    in_specs = (P(seq, "tp"), P(seq, "tp"), P(seq, "tp"), P(seq, "tp"), P("tp"), P(seq, "tp"))
    out_specs = (P(seq, "tp"), P(seq, "tp"), P(seq, "tp"), P(("z", "x", "tp"), None))
    return jax.shard_map(body, mesh=grid, in_specs=in_specs, out_specs=out_specs, check_vma=False)
```

```python
import jax
import numpy as np
import jax.numpy as jnp
from jax import lax
from jax.sharding import PartitionSpec as P

HEAD_DIM = 64
D_STATE = 256
SPAN = 128


precise = lax.Precision.HIGHEST


def prefix(part, axis, combine, identity, reverse):
    count = lax.axis_size(axis)
    place = lax.axis_index(axis)
    ahead = count - 1 - place if reverse else place
    gathered = jax.tree.map(lambda a: lax.all_gather(a, axis), part)
    state = jax.tree.map(lambda a, e: jnp.zeros_like(a) + jnp.asarray(e, a.dtype), part, identity)

    def one(turn, state):
        source = count - 1 - turn if reverse else turn
        return combine(
            state, jax.tree.map(lambda a: lax.dynamic_index_in_dim(a, source, 0, False), gathered)
        )

    return lax.fori_loop(0, ahead, one, state)


def exchange(values, axis):
    count = values.shape[0]
    place = lax.axis_index(axis)
    parts = [lax.dynamic_index_in_dim(values, place, 0, False)]
    for shift in range(1, count):
        chunk = lax.dynamic_index_in_dim(values, (place + shift) % count, 0, False)
        pairs = [(i, (i + shift) % count) for i in range(count)]
        parts.append(lax.ppermute(chunk, axis, pairs))
    got = jnp.stack(parts)
    return jnp.take(got, (place - jnp.arange(count)) % count, axis=0)


def seq_scan(device_log, device_fwd, device_bwd, axis):
    count = lax.axis_size(axis)
    place = lax.axis_index(axis)
    logs = device_log.reshape(-1)
    heads = logs.shape[0]
    stacked = jnp.stack([device_fwd, device_bwd]).transpose(0, 1, 3, 2, 4)
    shape = stacked.shape
    combos = 2 * heads
    if combos % count == 0:
        per = combos // count
        targets = np.arange(count)[:, None] * per + np.arange(per)[None, :]
        held = place * per + jnp.arange(per)
    else:
        per = 1
        targets = (np.arange(count) // (count // combos))[:, None]
        held = (place // (count // combos))[None]
    flat = stacked.reshape(count, per * 8, -1)
    width = flat.shape[2]
    tags = jnp.repeat(logs[targets % heads], 8, axis=1)
    tags = jnp.broadcast_to(tags[..., None], (count, per * 8, 128))
    payload = jnp.concatenate([flat, tags], axis=2)
    pieces = exchange(payload, axis)
    chosen = pieces[:, ::8, width]
    pieces = pieces[:, :, :width].reshape(count, per, -1)
    position = jnp.arange(count)
    low = jnp.minimum(position[:, None], position[None, :])
    high = jnp.maximum(position[:, None], position[None, :])
    between = ((position[None, None, :] > low[..., None]) & (position[None, None, :] < high[..., None]))
    exponent = jnp.einsum("ijm,mc->cij", between.astype(jnp.float32), chosen, precision=precise)
    before = (position[None, :] < position[:, None])
    after = (position[None, :] > position[:, None])
    mask = jnp.where((held < heads)[:, None, None], before[None], after[None])
    weights = jnp.where(mask, jnp.exp(exponent), 0.0)
    scanned = jnp.einsum("cij,jcx->icx", weights, pieces, precision=precise)
    back = exchange(scanned.reshape(count, per * 8, -1), axis)
    back = back.reshape(shape).transpose(0, 1, 3, 2, 4)
    return back[0], back[1]

def summarize(inputs, out_grad, input_proj, readout, step_size, decay_rate):
    cumulative = jnp.cumsum(-decay_rate[None] * step_size, axis=0)
    totals = cumulative[-1]
    to_end = jnp.exp(totals[None] - cumulative) * step_size
    forward = jnp.einsum(
        "qghp,qgn->gnhp",
        inputs.astype(jnp.float32) * to_end[..., None],
        input_proj.astype(jnp.float32),
        precision=precise,
    )
    from_start = jnp.exp(cumulative)
    backward = jnp.einsum(
        "qghp,qgn->gnhp",
        out_grad.astype(jnp.float32) * from_start[..., None],
        readout.astype(jnp.float32),
        precision=precise,
    )
    return (totals, forward, backward)


def span_local(inputs_raw, out_raw, proj_raw, read_raw, step_size, decay_rate):
    inputs = inputs_raw.astype(jnp.float32)
    out_grad = out_raw.astype(jnp.float32)
    input_proj = proj_raw.astype(jnp.float32)
    readout = read_raw.astype(jnp.float32)
    length = inputs.shape[0]
    position = jnp.arange(length)
    causal = (position[:, None] >= position[None, :]).astype(jnp.float32)
    cumulative = jnp.cumsum(-decay_rate[None] * step_size, axis=0)
    totals = cumulative[-1]
    spread = cumulative[:, None] - cumulative[None, :]
    decays = jnp.exp(jnp.minimum(spread, 0.0)) * causal[:, :, None, None]
    to_end = jnp.exp(totals[None] - cumulative)
    from_start = jnp.exp(cumulative)
    state_match = jnp.einsum("ugn,sgn->usg", read_raw, proj_raw, preferred_element_type=jnp.float32)
    grad_match = jnp.einsum(
        "ughp,sghp->usgh", out_raw, inputs_raw, preferred_element_type=jnp.float32
    )
    mix_input = decays * state_match[..., None]
    vector = jnp.einsum("usgh,ughp->sghp", mix_input, out_grad, precision=precise)
    direct = jnp.sum(inputs * vector, axis=-1)
    mix_state = decays * grad_match * step_size[None]
    grad_proj = jnp.einsum("usgh,ugn->sgn", mix_state, readout, precision=precise)
    grad_read = jnp.einsum("usgh,sgn->ugn", mix_state, input_proj, precision=precise)
    weights = mix_state * state_match[..., None]
    exclusive = jnp.cumsum(weights, axis=1) - weights
    paired = jnp.sum(exclusive * causal[:, :, None, None], axis=0)
    return (vector, direct, grad_proj, grad_read, paired)


def span_state(
    inputs_raw, out_raw, proj_raw, read_raw, step_size, decay_rate, state_in, grad_in, local
):
    vector, direct, grad_proj, grad_read, paired = local
    inputs = inputs_raw.astype(jnp.float32)
    out_grad = out_raw.astype(jnp.float32)
    input_proj = proj_raw.astype(jnp.float32)
    readout = read_raw.astype(jnp.float32)
    length = inputs.shape[0]
    position = jnp.arange(length)
    causal = (position[:, None] >= position[None, :]).astype(jnp.float32)
    strictly = (position[:, None] < position[None, :]).astype(jnp.float32)
    cumulative = jnp.cumsum(-decay_rate[None] * step_size, axis=0)
    totals = cumulative[-1]
    to_end = jnp.exp(totals[None] - cumulative)
    from_start = jnp.exp(cumulative)
    back_b = jnp.einsum("gnhp,sgn->sghp", grad_in, input_proj, precision=precise)
    vector = vector + to_end[..., None] * back_b
    grad_inputs = step_size[..., None] * vector
    tail_dot = jnp.sum(inputs * back_b, axis=-1)
    direct = direct + to_end * tail_dot
    scaled_x = (step_size * to_end)[..., None] * inputs
    grad_proj = grad_proj + jnp.einsum("sghp,gnhp->sgn", scaled_x, grad_in, precision=precise)
    scaled_y = from_start[..., None] * out_grad
    grad_read = grad_read + jnp.einsum("ughp,gnhp->ugn", scaled_y, state_in, precision=precise)
    read_state = jnp.einsum("ugn,gnhp->ughp", readout, state_in, precision=precise)
    from_init = from_start * jnp.sum(read_state * out_grad, axis=-1)
    suffixes = jnp.einsum("ut,ugh->tgh", causal, from_init, precision=precise)
    from_tail = to_end * step_size * tail_dot
    prefixes = jnp.einsum("st,sgh->tgh", strictly, from_tail, precision=precise)
    constant = jnp.exp(totals) * jnp.einsum("gnhp,gnhp->gh", grad_in, state_in, precision=precise)
    grad_log = paired + suffixes + prefixes + constant[None]
    grad_step = direct - decay_rate[None] * grad_log
    return (grad_inputs, grad_proj, grad_read, grad_step)


def combine(earlier, later):
    return (earlier[0] + later[0], jnp.exp(later[0])[:, None, :, None] * earlier[1] + later[1])


def span_prefix(log_sums, states, reverse):
    initial = (jnp.zeros_like(log_sums[0]), jnp.zeros_like(states[0]))

    def advance(carried, element):
        return (combine(carried, element), carried)

    return lax.scan(advance, initial, (log_sums, states), reverse=reverse)


def to_spans(
    inputs, out_grad, input_proj, readout, step_size, group_count, state_dim, head_dim, span_len
):
    span_count = inputs.shape[0] // span_len
    head_count = step_size.shape[1] // group_count
    return (
        inputs.reshape(span_count, span_len, group_count, head_count, head_dim),
        out_grad.reshape(span_count, span_len, group_count, head_count, head_dim),
        input_proj.reshape(span_count, span_len, group_count, state_dim),
        readout.reshape(span_count, span_len, group_count, state_dim),
        step_size.reshape(span_count, span_len, group_count, head_count),
    )


def over_spans(function, items):
    if jax.tree.leaves(items)[0].shape[0] == 1:
        return jax.tree.map(lambda a: a[None], function(jax.tree.map(lambda a: a[0], items)))
    return lax.map(function, items)


def body(inputs, input_proj, readout, step_size, decay_rate, out_grad):
    group_count = input_proj.shape[1] // D_STATE
    blocks = to_spans(
        inputs, out_grad, input_proj, readout, step_size, group_count, D_STATE, HEAD_DIM, SPAN
    )
    rate_rows = decay_rate.reshape(group_count, -1)
    totals, forward, backward = over_spans(lambda e: summarize(*e, rate_rows), blocks)
    if totals.shape[0] == 1:
        device_log, device_fwd, device_bwd = totals[0], forward[0], backward[0]
        log_before = log_after = jnp.zeros_like(totals)
        fwd_before = bwd_after = jnp.zeros_like(forward)
    else:
        (device_log, device_fwd), (log_before, fwd_before) = span_prefix(totals, forward, False)
        (ignored_log, device_bwd), (log_after, bwd_after) = span_prefix(totals, backward, True)
    local = over_spans(lambda e: span_local(*e, rate_rows), blocks)
    device_in, device_out = seq_scan(device_log, device_fwd, device_bwd, "seq")
    state_ins = fwd_before + jnp.exp(log_before)[:, :, None, :, None] * device_in[None]
    grad_ins = bwd_after + jnp.exp(log_after)[:, :, None, :, None] * device_out[None]
    gradients = over_spans(
        lambda e: span_state(*e[0], rate_rows, e[1], e[2], e[3]),
        (blocks, state_ins, grad_ins, local),
    )
    tokens = gradients[0].shape[0] * gradients[0].shape[1]
    grad_inputs, grad_proj, grad_read, grad_step = (g.reshape(tokens, -1) for g in gradients)
    regrouped = lax.all_to_all(grad_step, "tp", split_axis=0, concat_axis=1, tiled=True)
    return (
        grad_inputs.astype(jnp.bfloat16),
        grad_proj.astype(jnp.bfloat16),
        grad_read.astype(jnp.bfloat16),
        regrouped,
    )


def solution(mesh):
    in_specs = (
        P("seq", "tp"),
        P("seq", "tp"),
        P("seq", "tp"),
        P("seq", "tp"),
        P("tp"),
        P("seq", "tp"),
    )
    out_specs = (P("seq", "tp"), P("seq", "tp"), P("seq", "tp"), P(("seq", "tp"), None))
    return jax.shard_map(body, mesh=mesh, in_specs=in_specs, out_specs=out_specs, check_vma=False)
```

```python
import jax
import numpy as np
import jax.numpy as jnp
from jax import lax
from jax.sharding import PartitionSpec as P

HEAD_DIM = 64
D_STATE = 256
SPAN = 128


precise = lax.Precision.HIGHEST


def prefix(part, axis, combine, identity, reverse):
    count = lax.axis_size(axis)
    place = lax.axis_index(axis)
    ahead = count - 1 - place if reverse else place
    gathered = jax.tree.map(lambda a: lax.all_gather(a, axis), part)
    state = jax.tree.map(lambda a, e: jnp.zeros_like(a) + jnp.asarray(e, a.dtype), part, identity)

    def one(turn, state):
        source = count - 1 - turn if reverse else turn
        return combine(
            state, jax.tree.map(lambda a: lax.dynamic_index_in_dim(a, source, 0, False), gathered)
        )

    return lax.fori_loop(0, ahead, one, state)


def seq_scan(device_log, device_fwd, device_bwd, axis):
    count = lax.axis_size(axis)
    place = lax.axis_index(axis)
    group_count, state_dim, heads, head_dim = device_fwd.shape
    stacked = jnp.stack([device_fwd, device_bwd])
    shape = stacked.shape
    rows = 2 * group_count * state_dim // count
    block = (place * rows) // state_dim
    forward = block < group_count
    group = block % group_count
    flat = stacked.reshape(count, rows, heads * head_dim)
    width = flat.shape[2]
    owner = (np.arange(count) * rows // state_dim) % group_count
    tags = jnp.pad(device_log[owner], ((0, 0), (0, 128 - heads)))
    tags = jnp.broadcast_to(tags[:, None, :], (count, rows, 128))
    payload = jnp.concatenate([flat, tags], axis=2)
    pieces = lax.all_to_all(payload, axis, 0, 0, tiled=True)
    chosen = pieces[:, 0, width : width + heads]
    pieces = pieces[:, :, :width].reshape(count, rows, heads, head_dim)
    position = jnp.arange(count)
    low = jnp.minimum(position[:, None], position[None, :])
    high = jnp.maximum(position[:, None], position[None, :])
    between = ((position[None, None, :] > low[..., None]) & (position[None, None, :] < high[..., None]))
    exponent = jnp.einsum("ijm,mh->hij", between.astype(jnp.float32), chosen, precision=precise)
    before = (position[None, :] < position[:, None])
    after = (position[None, :] > position[:, None])
    mask = jnp.where(forward, before, after)
    weights = jnp.where(mask[None], jnp.exp(exponent), 0.0)
    scanned = jnp.einsum("hij,jrhp->irhp", weights, pieces, precision=precise)
    back = lax.all_to_all(scanned.reshape(count, rows, width), axis, 0, 0, tiled=True)
    back = back.reshape(shape)
    return back[0], back[1]

def summarize(inputs, out_grad, input_proj, readout, step_size, decay_rate):
    cumulative = jnp.cumsum(-decay_rate[None] * step_size, axis=0)
    totals = cumulative[-1]
    to_end = jnp.exp(totals[None] - cumulative) * step_size
    forward = jnp.einsum(
        "qghp,qgn->gnhp",
        inputs.astype(jnp.float32) * to_end[..., None],
        input_proj.astype(jnp.float32),
        precision=precise,
    )
    from_start = jnp.exp(cumulative)
    backward = jnp.einsum(
        "qghp,qgn->gnhp",
        out_grad.astype(jnp.float32) * from_start[..., None],
        readout.astype(jnp.float32),
        precision=precise,
    )
    return (totals, forward, backward)


def span_local(inputs_raw, out_raw, proj_raw, read_raw, step_size, decay_rate):
    inputs = inputs_raw.astype(jnp.float32)
    out_grad = out_raw.astype(jnp.float32)
    input_proj = proj_raw.astype(jnp.float32)
    readout = read_raw.astype(jnp.float32)
    length = inputs.shape[0]
    position = jnp.arange(length)
    causal = (position[:, None] >= position[None, :]).astype(jnp.float32)
    cumulative = jnp.cumsum(-decay_rate[None] * step_size, axis=0)
    totals = cumulative[-1]
    spread = cumulative[:, None] - cumulative[None, :]
    decays = jnp.exp(jnp.minimum(spread, 0.0)) * causal[:, :, None, None]
    to_end = jnp.exp(totals[None] - cumulative)
    from_start = jnp.exp(cumulative)
    state_match = jnp.einsum("ugn,sgn->usg", read_raw, proj_raw, preferred_element_type=jnp.float32)
    grad_match = jnp.einsum(
        "ughp,sghp->usgh", out_raw, inputs_raw, preferred_element_type=jnp.float32
    )
    mix_input = decays * state_match[..., None]
    vector = jnp.einsum("usgh,ughp->sghp", mix_input, out_grad, precision=precise)
    direct = jnp.sum(inputs * vector, axis=-1)
    mix_state = decays * grad_match * step_size[None]
    grad_proj = jnp.einsum("usgh,ugn->sgn", mix_state, readout, precision=precise)
    grad_read = jnp.einsum("usgh,sgn->ugn", mix_state, input_proj, precision=precise)
    weights = mix_state * state_match[..., None]
    exclusive = jnp.cumsum(weights, axis=1) - weights
    paired = jnp.sum(exclusive * causal[:, :, None, None], axis=0)
    return (vector, direct, grad_proj, grad_read, paired)


def span_state(
    inputs_raw, out_raw, proj_raw, read_raw, step_size, decay_rate, state_in, grad_in, local
):
    vector, direct, grad_proj, grad_read, paired = local
    inputs = inputs_raw.astype(jnp.float32)
    out_grad = out_raw.astype(jnp.float32)
    input_proj = proj_raw.astype(jnp.float32)
    readout = read_raw.astype(jnp.float32)
    length = inputs.shape[0]
    position = jnp.arange(length)
    causal = (position[:, None] >= position[None, :]).astype(jnp.float32)
    strictly = (position[:, None] < position[None, :]).astype(jnp.float32)
    cumulative = jnp.cumsum(-decay_rate[None] * step_size, axis=0)
    totals = cumulative[-1]
    to_end = jnp.exp(totals[None] - cumulative)
    from_start = jnp.exp(cumulative)
    back_b = jnp.einsum("gnhp,sgn->sghp", grad_in, input_proj, precision=precise)
    vector = vector + to_end[..., None] * back_b
    grad_inputs = step_size[..., None] * vector
    tail_dot = jnp.sum(inputs * back_b, axis=-1)
    direct = direct + to_end * tail_dot
    scaled_x = (step_size * to_end)[..., None] * inputs
    grad_proj = grad_proj + jnp.einsum("sghp,gnhp->sgn", scaled_x, grad_in, precision=precise)
    scaled_y = from_start[..., None] * out_grad
    grad_read = grad_read + jnp.einsum("ughp,gnhp->ugn", scaled_y, state_in, precision=precise)
    read_state = jnp.einsum("ugn,gnhp->ughp", readout, state_in, precision=precise)
    from_init = from_start * jnp.sum(read_state * out_grad, axis=-1)
    suffixes = jnp.einsum("ut,ugh->tgh", causal, from_init, precision=precise)
    from_tail = to_end * step_size * tail_dot
    prefixes = jnp.einsum("st,sgh->tgh", strictly, from_tail, precision=precise)
    constant = jnp.exp(totals) * jnp.einsum("gnhp,gnhp->gh", grad_in, state_in, precision=precise)
    grad_log = paired + suffixes + prefixes + constant[None]
    grad_step = direct - decay_rate[None] * grad_log
    return (grad_inputs, grad_proj, grad_read, grad_step)


def combine(earlier, later):
    return (earlier[0] + later[0], jnp.exp(later[0])[:, None, :, None] * earlier[1] + later[1])


def span_prefix(log_sums, states, reverse):
    initial = (jnp.zeros_like(log_sums[0]), jnp.zeros_like(states[0]))

    def advance(carried, element):
        return (combine(carried, element), carried)

    return lax.scan(advance, initial, (log_sums, states), reverse=reverse)


def to_spans(
    inputs, out_grad, input_proj, readout, step_size, group_count, state_dim, head_dim, span_len
):
    span_count = inputs.shape[0] // span_len
    head_count = step_size.shape[1] // group_count
    return (
        inputs.reshape(span_count, span_len, group_count, head_count, head_dim),
        out_grad.reshape(span_count, span_len, group_count, head_count, head_dim),
        input_proj.reshape(span_count, span_len, group_count, state_dim),
        readout.reshape(span_count, span_len, group_count, state_dim),
        step_size.reshape(span_count, span_len, group_count, head_count),
    )


def over_spans(function, items):
    if jax.tree.leaves(items)[0].shape[0] == 1:
        return jax.tree.map(lambda a: a[None], function(jax.tree.map(lambda a: a[0], items)))
    return lax.map(function, items)


def body(inputs, input_proj, readout, step_size, decay_rate, out_grad):
    group_count = input_proj.shape[1] // D_STATE
    blocks = to_spans(
        inputs, out_grad, input_proj, readout, step_size, group_count, D_STATE, HEAD_DIM, SPAN
    )
    rate_rows = decay_rate.reshape(group_count, -1)
    totals, forward, backward = over_spans(lambda e: summarize(*e, rate_rows), blocks)
    if totals.shape[0] == 1:
        device_log, device_fwd, device_bwd = totals[0], forward[0], backward[0]
        log_before = log_after = jnp.zeros_like(totals)
        fwd_before = bwd_after = jnp.zeros_like(forward)
    else:
        (device_log, device_fwd), (log_before, fwd_before) = span_prefix(totals, forward, False)
        (ignored_log, device_bwd), (log_after, bwd_after) = span_prefix(totals, backward, True)
    local = over_spans(lambda e: span_local(*e, rate_rows), blocks)
    device_in, device_out = seq_scan(device_log, device_fwd, device_bwd, "seq")
    state_ins = fwd_before + jnp.exp(log_before)[:, :, None, :, None] * device_in[None]
    grad_ins = bwd_after + jnp.exp(log_after)[:, :, None, :, None] * device_out[None]
    gradients = over_spans(
        lambda e: span_state(*e[0], rate_rows, e[1], e[2], e[3]),
        (blocks, state_ins, grad_ins, local),
    )
    tokens = gradients[0].shape[0] * gradients[0].shape[1]
    grad_inputs, grad_proj, grad_read, grad_step = (g.reshape(tokens, -1) for g in gradients)
    regrouped = lax.all_to_all(grad_step, "tp", split_axis=0, concat_axis=1, tiled=True)
    return (
        grad_inputs.astype(jnp.bfloat16),
        grad_proj.astype(jnp.bfloat16),
        grad_read.astype(jnp.bfloat16),
        regrouped,
    )


def solution(mesh):
    in_specs = (
        P("seq", "tp"),
        P("seq", "tp"),
        P("seq", "tp"),
        P("seq", "tp"),
        P("tp"),
        P("seq", "tp"),
    )
    out_specs = (P("seq", "tp"), P("seq", "tp"), P("seq", "tp"), P(("seq", "tp"), None))
    return jax.shard_map(body, mesh=mesh, in_specs=in_specs, out_specs=out_specs, check_vma=False)
```

```python
import jax
import numpy as np
import jax.numpy as jnp
from jax import lax
from jax.sharding import PartitionSpec as P

HEAD_DIM = 64
D_STATE = 256
SPAN = 128


precise = lax.Precision.HIGHEST
fast = lax.Precision.HIGH


def prefix(part, axis, combine, identity, reverse):
    count = lax.axis_size(axis)
    place = lax.axis_index(axis)
    ahead = count - 1 - place if reverse else place
    gathered = jax.tree.map(lambda a: lax.all_gather(a, axis), part)
    state = jax.tree.map(lambda a, e: jnp.zeros_like(a) + jnp.asarray(e, a.dtype), part, identity)

    def one(turn, state):
        source = count - 1 - turn if reverse else turn
        return combine(
            state, jax.tree.map(lambda a: lax.dynamic_index_in_dim(a, source, 0, False), gathered)
        )

    return lax.fori_loop(0, ahead, one, state)


def seq_scan(device_log, device_fwd, device_bwd, axis):
    count = lax.axis_size(axis)
    place = lax.axis_index(axis)
    logs = device_log.reshape(-1)
    heads = logs.shape[0]
    stacked = jnp.stack([device_fwd, device_bwd]).transpose(0, 1, 3, 2, 4)
    shape = stacked.shape
    combos = 2 * heads
    if combos % count == 0:
        per = combos // count
        targets = np.arange(count)[:, None] * per + np.arange(per)[None, :]
        held = place * per + jnp.arange(per)
    else:
        per = 1
        targets = (np.arange(count) // (count // combos))[:, None]
        held = (place // (count // combos))[None]
    flat = stacked.reshape(count, per * 8, -1)
    width = flat.shape[2]
    tags = jnp.repeat(logs[targets % heads], 8, axis=1)
    tags = jnp.broadcast_to(tags[..., None], (count, per * 8, 128))
    payload = jnp.concatenate([flat, tags], axis=2)
    pieces = lax.all_to_all(payload, axis, 0, 0, tiled=True)
    chosen = pieces[:, ::8, width]
    pieces = pieces[:, :, :width].reshape(count, per, -1)
    position = jnp.arange(count)
    low = jnp.minimum(position[:, None], position[None, :])
    high = jnp.maximum(position[:, None], position[None, :])
    between = ((position[None, None, :] > low[..., None]) & (position[None, None, :] < high[..., None]))
    exponent = jnp.einsum("ijm,mc->cij", between.astype(jnp.float32), chosen, precision=precise)
    before = (position[None, :] < position[:, None])
    after = (position[None, :] > position[:, None])
    mask = jnp.where((held < heads)[:, None, None], before[None], after[None])
    weights = jnp.where(mask, jnp.exp(exponent), 0.0)
    scanned = jnp.einsum("cij,jcx->icx", weights, pieces, precision=fast)
    back = lax.all_to_all(scanned.reshape(count, per * 8, -1), axis, 0, 0, tiled=True)
    back = back.reshape(shape).transpose(0, 1, 3, 2, 4)
    return back[0], back[1]

def summarize(inputs, out_grad, input_proj, readout, step_size, decay_rate):
    cumulative = jnp.cumsum(-decay_rate[None] * step_size, axis=0)
    totals = cumulative[-1]
    to_end = jnp.exp(totals[None] - cumulative) * step_size
    forward = jnp.einsum(
        "qghp,qgn->gnhp",
        inputs.astype(jnp.float32) * to_end[..., None],
        input_proj.astype(jnp.float32),
        precision=fast,
    )
    from_start = jnp.exp(cumulative)
    backward = jnp.einsum(
        "qghp,qgn->gnhp",
        out_grad.astype(jnp.float32) * from_start[..., None],
        readout.astype(jnp.float32),
        precision=fast,
    )
    return (totals, forward, backward)


def span_local(inputs_raw, out_raw, proj_raw, read_raw, step_size, decay_rate):
    inputs = inputs_raw.astype(jnp.float32)
    out_grad = out_raw.astype(jnp.float32)
    input_proj = proj_raw.astype(jnp.float32)
    readout = read_raw.astype(jnp.float32)
    length = inputs.shape[0]
    position = jnp.arange(length)
    causal = (position[:, None] >= position[None, :]).astype(jnp.float32)
    cumulative = jnp.cumsum(-decay_rate[None] * step_size, axis=0)
    totals = cumulative[-1]
    spread = cumulative[:, None] - cumulative[None, :]
    decays = jnp.exp(jnp.minimum(spread, 0.0)) * causal[:, :, None, None]
    to_end = jnp.exp(totals[None] - cumulative)
    from_start = jnp.exp(cumulative)
    state_match = jnp.einsum("ugn,sgn->usg", read_raw, proj_raw, preferred_element_type=jnp.float32)
    grad_match = jnp.einsum(
        "ughp,sghp->usgh", out_raw, inputs_raw, preferred_element_type=jnp.float32
    )
    mix_input = decays * state_match[..., None]
    vector = jnp.einsum("usgh,ughp->sghp", mix_input, out_grad, precision=fast)
    direct = jnp.sum(inputs * vector, axis=-1)
    mix_state = decays * grad_match * step_size[None]
    grad_proj = jnp.einsum("usgh,ugn->sgn", mix_state, readout, precision=fast)
    grad_read = jnp.einsum("usgh,sgn->ugn", mix_state, input_proj, precision=fast)
    weights = mix_state * state_match[..., None]
    exclusive = jnp.cumsum(weights, axis=1) - weights
    paired = jnp.sum(exclusive * causal[:, :, None, None], axis=0)
    return (vector, direct, grad_proj, grad_read, paired)


def span_state(
    inputs_raw, out_raw, proj_raw, read_raw, step_size, decay_rate, state_in, grad_in, local
):
    vector, direct, grad_proj, grad_read, paired = local
    inputs = inputs_raw.astype(jnp.float32)
    out_grad = out_raw.astype(jnp.float32)
    input_proj = proj_raw.astype(jnp.float32)
    readout = read_raw.astype(jnp.float32)
    length = inputs.shape[0]
    position = jnp.arange(length)
    causal = (position[:, None] >= position[None, :]).astype(jnp.float32)
    strictly = (position[:, None] < position[None, :]).astype(jnp.float32)
    cumulative = jnp.cumsum(-decay_rate[None] * step_size, axis=0)
    totals = cumulative[-1]
    to_end = jnp.exp(totals[None] - cumulative)
    from_start = jnp.exp(cumulative)
    back_b = jnp.einsum("gnhp,sgn->sghp", grad_in, input_proj, precision=fast)
    vector = vector + to_end[..., None] * back_b
    grad_inputs = step_size[..., None] * vector
    tail_dot = jnp.sum(inputs * back_b, axis=-1)
    direct = direct + to_end * tail_dot
    scaled_x = (step_size * to_end)[..., None] * inputs
    grad_proj = grad_proj + jnp.einsum("sghp,gnhp->sgn", scaled_x, grad_in, precision=fast)
    scaled_y = from_start[..., None] * out_grad
    grad_read = grad_read + jnp.einsum("ughp,gnhp->ugn", scaled_y, state_in, precision=fast)
    read_state = jnp.einsum("ugn,gnhp->ughp", readout, state_in, precision=fast)
    from_init = from_start * jnp.sum(read_state * out_grad, axis=-1)
    suffixes = jnp.einsum("ut,ugh->tgh", causal, from_init, precision=fast)
    from_tail = to_end * step_size * tail_dot
    prefixes = jnp.einsum("st,sgh->tgh", strictly, from_tail, precision=fast)
    constant = jnp.exp(totals) * jnp.einsum("gnhp,gnhp->gh", grad_in, state_in, precision=fast)
    grad_log = paired + suffixes + prefixes + constant[None]
    grad_step = direct - decay_rate[None] * grad_log
    return (grad_inputs, grad_proj, grad_read, grad_step)


def combine(earlier, later):
    return (earlier[0] + later[0], jnp.exp(later[0])[:, None, :, None] * earlier[1] + later[1])


def span_prefix(log_sums, states, reverse):
    initial = (jnp.zeros_like(log_sums[0]), jnp.zeros_like(states[0]))

    def advance(carried, element):
        return (combine(carried, element), carried)

    return lax.scan(advance, initial, (log_sums, states), reverse=reverse)


def to_spans(
    inputs, out_grad, input_proj, readout, step_size, group_count, state_dim, head_dim, span_len
):
    span_count = inputs.shape[0] // span_len
    head_count = step_size.shape[1] // group_count
    return (
        inputs.reshape(span_count, span_len, group_count, head_count, head_dim),
        out_grad.reshape(span_count, span_len, group_count, head_count, head_dim),
        input_proj.reshape(span_count, span_len, group_count, state_dim),
        readout.reshape(span_count, span_len, group_count, state_dim),
        step_size.reshape(span_count, span_len, group_count, head_count),
    )


def over_spans(function, items):
    if jax.tree.leaves(items)[0].shape[0] == 1:
        return jax.tree.map(lambda a: a[None], function(jax.tree.map(lambda a: a[0], items)))
    return lax.map(function, items)


def body(inputs, input_proj, readout, step_size, decay_rate, out_grad):
    group_count = input_proj.shape[1] // D_STATE
    blocks = to_spans(
        inputs, out_grad, input_proj, readout, step_size, group_count, D_STATE, HEAD_DIM, SPAN
    )
    rate_rows = decay_rate.reshape(group_count, -1)
    totals, forward, backward = over_spans(lambda e: summarize(*e, rate_rows), blocks)
    if totals.shape[0] == 1:
        device_log, device_fwd, device_bwd = totals[0], forward[0], backward[0]
        log_before = log_after = jnp.zeros_like(totals)
        fwd_before = bwd_after = jnp.zeros_like(forward)
    else:
        (device_log, device_fwd), (log_before, fwd_before) = span_prefix(totals, forward, False)
        (ignored_log, device_bwd), (log_after, bwd_after) = span_prefix(totals, backward, True)
    local = over_spans(lambda e: span_local(*e, rate_rows), blocks)
    device_in, device_out = seq_scan(device_log, device_fwd, device_bwd, "seq")
    state_ins = fwd_before + jnp.exp(log_before)[:, :, None, :, None] * device_in[None]
    grad_ins = bwd_after + jnp.exp(log_after)[:, :, None, :, None] * device_out[None]
    gradients = over_spans(
        lambda e: span_state(*e[0], rate_rows, e[1], e[2], e[3]),
        (blocks, state_ins, grad_ins, local),
    )
    tokens = gradients[0].shape[0] * gradients[0].shape[1]
    grad_inputs, grad_proj, grad_read, grad_step = (g.reshape(tokens, -1) for g in gradients)
    regrouped = lax.all_to_all(grad_step, "tp", split_axis=0, concat_axis=1, tiled=True)
    return (
        grad_inputs.astype(jnp.bfloat16),
        grad_proj.astype(jnp.bfloat16),
        grad_read.astype(jnp.bfloat16),
        regrouped,
    )


def solution(mesh):
    in_specs = (
        P("seq", "tp"),
        P("seq", "tp"),
        P("seq", "tp"),
        P("seq", "tp"),
        P("tp"),
        P("seq", "tp"),
    )
    out_specs = (P("seq", "tp"), P("seq", "tp"), P("seq", "tp"), P(("seq", "tp"), None))
    return jax.shard_map(body, mesh=mesh, in_specs=in_specs, out_specs=out_specs, check_vma=False)
```

```python
import jax
import numpy as np
import jax.numpy as jnp
from jax import lax
from jax.sharding import PartitionSpec as P

HEAD_DIM = 64
D_STATE = 256
SPAN = 128


precise = lax.Precision.HIGHEST
fast = lax.Precision.HIGH


def prefix(part, axis, combine, identity, reverse):
    count = lax.axis_size(axis)
    place = lax.axis_index(axis)
    ahead = count - 1 - place if reverse else place
    gathered = jax.tree.map(lambda a: lax.all_gather(a, axis), part)
    state = jax.tree.map(lambda a, e: jnp.zeros_like(a) + jnp.asarray(e, a.dtype), part, identity)

    def one(turn, state):
        source = count - 1 - turn if reverse else turn
        return combine(
            state, jax.tree.map(lambda a: lax.dynamic_index_in_dim(a, source, 0, False), gathered)
        )

    return lax.fori_loop(0, ahead, one, state)


def seq_scan(device_log, device_fwd, device_bwd, axis):
    count = lax.axis_size(axis)
    place = lax.axis_index(axis)
    group_count, state_dim, heads, head_dim = device_fwd.shape
    tiles = heads * head_dim // 128
    per_tile = 128 // head_dim
    halves = count // (2 * group_count * tiles)
    rows = state_dim // halves
    stacked = jnp.stack([device_fwd, device_bwd])
    shape = stacked.shape
    cut = stacked.reshape(2, group_count, halves, rows, tiles, 128).transpose(0, 1, 4, 2, 3, 5)
    cut = cut.reshape(count, rows, 128)
    index = np.arange(count)
    owner_group = (index // (tiles * halves)) % group_count
    owner_tile = (index // halves) % tiles
    owned = owner_tile[:, None] * per_tile + np.arange(per_tile)[None, :]
    tags = jnp.pad(device_log[owner_group[:, None], owned], ((0, 0), (0, 128 - per_tile)))
    tags = jnp.broadcast_to(tags[:, None, :], (count, 8, 128))
    got = lax.all_to_all(jnp.concatenate([cut, tags], axis=1), axis, 0, 0, tiled=True)
    chosen = got[:, rows, :per_tile]
    pieces = got[:, :rows, :]
    forward = place < count // 2
    position = jnp.arange(count)
    low = jnp.minimum(position[:, None], position[None, :])
    high = jnp.maximum(position[:, None], position[None, :])
    between = ((position[None, None, :] > low[..., None]) & (position[None, None, :] < high[..., None]))
    exponent = jnp.einsum("ijm,mc->cij", between.astype(jnp.float32), chosen, precision=precise)
    before = (position[None, :] < position[:, None])
    after = (position[None, :] > position[:, None])
    mask = jnp.where(forward, before, after)
    weights = jnp.where(mask[None], jnp.exp(exponent), 0.0)
    lane_head = np.arange(128) // head_dim
    scanned = jnp.zeros_like(pieces)
    for head in range(per_tile):
        part = jnp.einsum("ij,jrl->irl", weights[head], pieces, precision=fast)
        scanned = jnp.where(lane_head == head, part, scanned)
    back = lax.all_to_all(scanned, axis, 0, 0, tiled=True)
    back = back.reshape(2, group_count, tiles, halves, rows, 128).transpose(0, 1, 3, 4, 2, 5)
    back = back.reshape(shape)
    return back[0], back[1]

def summarize(inputs, out_grad, input_proj, readout, step_size, decay_rate):
    cumulative = jnp.cumsum(-decay_rate[None] * step_size, axis=0)
    totals = cumulative[-1]
    to_end = jnp.exp(totals[None] - cumulative) * step_size
    forward = jnp.einsum(
        "qghp,qgn->gnhp",
        inputs.astype(jnp.float32) * to_end[..., None],
        input_proj.astype(jnp.float32),
        precision=fast,
    )
    from_start = jnp.exp(cumulative)
    backward = jnp.einsum(
        "qghp,qgn->gnhp",
        out_grad.astype(jnp.float32) * from_start[..., None],
        readout.astype(jnp.float32),
        precision=fast,
    )
    return (totals, forward, backward)


def span_local(inputs_raw, out_raw, proj_raw, read_raw, step_size, decay_rate):
    inputs = inputs_raw.astype(jnp.float32)
    out_grad = out_raw.astype(jnp.float32)
    input_proj = proj_raw.astype(jnp.float32)
    readout = read_raw.astype(jnp.float32)
    length = inputs.shape[0]
    position = jnp.arange(length)
    causal = (position[:, None] >= position[None, :]).astype(jnp.float32)
    cumulative = jnp.cumsum(-decay_rate[None] * step_size, axis=0)
    totals = cumulative[-1]
    spread = cumulative[:, None] - cumulative[None, :]
    decays = jnp.exp(jnp.minimum(spread, 0.0)) * causal[:, :, None, None]
    to_end = jnp.exp(totals[None] - cumulative)
    from_start = jnp.exp(cumulative)
    state_match = jnp.einsum("ugn,sgn->usg", read_raw, proj_raw, preferred_element_type=jnp.float32)
    grad_match = jnp.einsum(
        "ughp,sghp->usgh", out_raw, inputs_raw, preferred_element_type=jnp.float32
    )
    mix_input = decays * state_match[..., None]
    vector = jnp.einsum("usgh,ughp->sghp", mix_input, out_grad, precision=fast)
    direct = jnp.sum(inputs * vector, axis=-1)
    mix_state = decays * grad_match * step_size[None]
    grad_proj = jnp.einsum("usgh,ugn->sgn", mix_state, readout, precision=fast)
    grad_read = jnp.einsum("usgh,sgn->ugn", mix_state, input_proj, precision=fast)
    weights = mix_state * state_match[..., None]
    exclusive = jnp.cumsum(weights, axis=1) - weights
    paired = jnp.sum(exclusive * causal[:, :, None, None], axis=0)
    return (vector, direct, grad_proj, grad_read, paired)


def span_state(
    inputs_raw, out_raw, proj_raw, read_raw, step_size, decay_rate, state_in, grad_in, local
):
    vector, direct, grad_proj, grad_read, paired = local
    inputs = inputs_raw.astype(jnp.float32)
    out_grad = out_raw.astype(jnp.float32)
    input_proj = proj_raw.astype(jnp.float32)
    readout = read_raw.astype(jnp.float32)
    length = inputs.shape[0]
    position = jnp.arange(length)
    causal = (position[:, None] >= position[None, :]).astype(jnp.float32)
    strictly = (position[:, None] < position[None, :]).astype(jnp.float32)
    cumulative = jnp.cumsum(-decay_rate[None] * step_size, axis=0)
    totals = cumulative[-1]
    to_end = jnp.exp(totals[None] - cumulative)
    from_start = jnp.exp(cumulative)
    back_b = jnp.einsum("gnhp,sgn->sghp", grad_in, input_proj, precision=fast)
    vector = vector + to_end[..., None] * back_b
    grad_inputs = step_size[..., None] * vector
    tail_dot = jnp.sum(inputs * back_b, axis=-1)
    direct = direct + to_end * tail_dot
    scaled_x = (step_size * to_end)[..., None] * inputs
    grad_proj = grad_proj + jnp.einsum("sghp,gnhp->sgn", scaled_x, grad_in, precision=fast)
    scaled_y = from_start[..., None] * out_grad
    grad_read = grad_read + jnp.einsum("ughp,gnhp->ugn", scaled_y, state_in, precision=fast)
    read_state = jnp.einsum("ugn,gnhp->ughp", readout, state_in, precision=fast)
    from_init = from_start * jnp.sum(read_state * out_grad, axis=-1)
    suffixes = jnp.einsum("ut,ugh->tgh", causal, from_init, precision=fast)
    from_tail = to_end * step_size * tail_dot
    prefixes = jnp.einsum("st,sgh->tgh", strictly, from_tail, precision=fast)
    constant = jnp.exp(totals) * jnp.einsum("gnhp,gnhp->gh", grad_in, state_in, precision=fast)
    grad_log = paired + suffixes + prefixes + constant[None]
    grad_step = direct - decay_rate[None] * grad_log
    return (grad_inputs, grad_proj, grad_read, grad_step)


def combine(earlier, later):
    return (earlier[0] + later[0], jnp.exp(later[0])[:, None, :, None] * earlier[1] + later[1])


def span_prefix(log_sums, states, reverse):
    initial = (jnp.zeros_like(log_sums[0]), jnp.zeros_like(states[0]))

    def advance(carried, element):
        return (combine(carried, element), carried)

    return lax.scan(advance, initial, (log_sums, states), reverse=reverse)


def to_spans(
    inputs, out_grad, input_proj, readout, step_size, group_count, state_dim, head_dim, span_len
):
    span_count = inputs.shape[0] // span_len
    head_count = step_size.shape[1] // group_count
    return (
        inputs.reshape(span_count, span_len, group_count, head_count, head_dim),
        out_grad.reshape(span_count, span_len, group_count, head_count, head_dim),
        input_proj.reshape(span_count, span_len, group_count, state_dim),
        readout.reshape(span_count, span_len, group_count, state_dim),
        step_size.reshape(span_count, span_len, group_count, head_count),
    )


def over_spans(function, items):
    if jax.tree.leaves(items)[0].shape[0] == 1:
        return jax.tree.map(lambda a: a[None], function(jax.tree.map(lambda a: a[0], items)))
    return lax.map(function, items)


def body(inputs, input_proj, readout, step_size, decay_rate, out_grad):
    group_count = input_proj.shape[1] // D_STATE
    blocks = to_spans(
        inputs, out_grad, input_proj, readout, step_size, group_count, D_STATE, HEAD_DIM, SPAN
    )
    rate_rows = decay_rate.reshape(group_count, -1)
    totals, forward, backward = over_spans(lambda e: summarize(*e, rate_rows), blocks)
    if totals.shape[0] == 1:
        device_log, device_fwd, device_bwd = totals[0], forward[0], backward[0]
        log_before = log_after = jnp.zeros_like(totals)
        fwd_before = bwd_after = jnp.zeros_like(forward)
    else:
        (device_log, device_fwd), (log_before, fwd_before) = span_prefix(totals, forward, False)
        (ignored_log, device_bwd), (log_after, bwd_after) = span_prefix(totals, backward, True)
    local = over_spans(lambda e: span_local(*e, rate_rows), blocks)
    device_in, device_out = seq_scan(device_log, device_fwd, device_bwd, "seq")
    state_ins = fwd_before + jnp.exp(log_before)[:, :, None, :, None] * device_in[None]
    grad_ins = bwd_after + jnp.exp(log_after)[:, :, None, :, None] * device_out[None]
    gradients = over_spans(
        lambda e: span_state(*e[0], rate_rows, e[1], e[2], e[3]),
        (blocks, state_ins, grad_ins, local),
    )
    tokens = gradients[0].shape[0] * gradients[0].shape[1]
    grad_inputs, grad_proj, grad_read, grad_step = (g.reshape(tokens, -1) for g in gradients)
    regrouped = lax.all_to_all(grad_step, "tp", split_axis=0, concat_axis=1, tiled=True)
    return (
        grad_inputs.astype(jnp.bfloat16),
        grad_proj.astype(jnp.bfloat16),
        grad_read.astype(jnp.bfloat16),
        regrouped,
    )


def solution(mesh):
    in_specs = (
        P("seq", "tp"),
        P("seq", "tp"),
        P("seq", "tp"),
        P("seq", "tp"),
        P("tp"),
        P("seq", "tp"),
    )
    out_specs = (P("seq", "tp"), P("seq", "tp"), P("seq", "tp"), P(("seq", "tp"), None))
    return jax.shard_map(body, mesh=mesh, in_specs=in_specs, out_specs=out_specs, check_vma=False)
```

```python
import jax
import numpy as np
import jax.numpy as jnp
from jax import lax
from jax.sharding import PartitionSpec as P

HEAD_DIM = 64
D_STATE = 256
SPAN = 128


precise = lax.Precision.HIGHEST
fast = lax.Precision.HIGH


def prefix(part, axis, combine, identity, reverse):
    count = lax.axis_size(axis)
    place = lax.axis_index(axis)
    ahead = count - 1 - place if reverse else place
    gathered = jax.tree.map(lambda a: lax.all_gather(a, axis), part)
    state = jax.tree.map(lambda a, e: jnp.zeros_like(a) + jnp.asarray(e, a.dtype), part, identity)

    def one(turn, state):
        source = count - 1 - turn if reverse else turn
        return combine(
            state, jax.tree.map(lambda a: lax.dynamic_index_in_dim(a, source, 0, False), gathered)
        )

    return lax.fori_loop(0, ahead, one, state)


def seq_scan(device_log, device_fwd, device_bwd, axis):
    count = lax.axis_size(axis)
    place = lax.axis_index(axis)
    logs = device_log.reshape(-1)
    heads = logs.shape[0]
    stacked = jnp.stack([device_fwd, device_bwd]).transpose(0, 1, 3, 4, 2)
    shape = stacked.shape
    head_dim, state_dim = shape[3], shape[4]
    combos = 2 * heads
    if combos % count == 0:
        per = combos // count
        targets = np.arange(count)[:, None] * per + np.arange(per)[None, :]
        held = place * per + jnp.arange(per)
    else:
        per = 1
        targets = (np.arange(count) // (count // combos))[:, None]
        held = (place // (count // combos))[None]
    tiled = (count, per, head_dim // 8, 8, state_dim // 128, 128)
    flat = stacked.reshape(tiled).transpose(0, 1, 2, 4, 3, 5).reshape(count, -1, 128)
    body_rows = flat.shape[1]
    tags = jnp.repeat(logs[targets % heads], 8, axis=1)
    tags = jnp.broadcast_to(tags[..., None], (count, per * 8, 128))
    payload = jnp.concatenate([flat, tags], axis=1)
    pieces = lax.all_to_all(payload, axis, 0, 0, tiled=True)
    chosen = pieces[:, body_rows::8, 0]
    pieces = pieces[:, :body_rows, :].reshape(count, per, -1)
    position = jnp.arange(count)
    low = jnp.minimum(position[:, None], position[None, :])
    high = jnp.maximum(position[:, None], position[None, :])
    between = ((position[None, None, :] > low[..., None]) & (position[None, None, :] < high[..., None]))
    exponent = jnp.einsum("ijm,mc->cij", between.astype(jnp.float32), chosen, precision=precise)
    before = (position[None, :] < position[:, None])
    after = (position[None, :] > position[:, None])
    mask = jnp.where((held < heads)[:, None, None], before[None], after[None])
    weights = jnp.where(mask, jnp.exp(exponent), 0.0)
    scanned = jnp.einsum("cij,jcx->icx", weights, pieces, precision=fast)
    back = lax.all_to_all(scanned.reshape(count, body_rows, 128), axis, 0, 0, tiled=True)
    back = back.reshape(count, per, head_dim // 8, state_dim // 128, 8, 128).transpose(0, 1, 2, 4, 3, 5)
    back = back.reshape(shape).transpose(0, 1, 4, 2, 3)
    return back[0], back[1]

def summarize(inputs, out_grad, input_proj, readout, step_size, decay_rate):
    cumulative = jnp.cumsum(-decay_rate[None] * step_size, axis=0)
    totals = cumulative[-1]
    to_end = jnp.exp(totals[None] - cumulative) * step_size
    forward = jnp.einsum(
        "qghp,qgn->gnhp",
        inputs.astype(jnp.float32) * to_end[..., None],
        input_proj.astype(jnp.float32),
        precision=fast,
    )
    from_start = jnp.exp(cumulative)
    backward = jnp.einsum(
        "qghp,qgn->gnhp",
        out_grad.astype(jnp.float32) * from_start[..., None],
        readout.astype(jnp.float32),
        precision=fast,
    )
    return (totals, forward, backward)


def span_local(inputs_raw, out_raw, proj_raw, read_raw, step_size, decay_rate):
    inputs = inputs_raw.astype(jnp.float32)
    out_grad = out_raw.astype(jnp.float32)
    input_proj = proj_raw.astype(jnp.float32)
    readout = read_raw.astype(jnp.float32)
    length = inputs.shape[0]
    position = jnp.arange(length)
    causal = (position[:, None] >= position[None, :]).astype(jnp.float32)
    cumulative = jnp.cumsum(-decay_rate[None] * step_size, axis=0)
    totals = cumulative[-1]
    spread = cumulative[:, None] - cumulative[None, :]
    decays = jnp.exp(jnp.minimum(spread, 0.0)) * causal[:, :, None, None]
    to_end = jnp.exp(totals[None] - cumulative)
    from_start = jnp.exp(cumulative)
    state_match = jnp.einsum("ugn,sgn->usg", read_raw, proj_raw, preferred_element_type=jnp.float32)
    grad_match = jnp.einsum(
        "ughp,sghp->usgh", out_raw, inputs_raw, preferred_element_type=jnp.float32
    )
    mix_input = decays * state_match[..., None]
    vector = jnp.einsum("usgh,ughp->sghp", mix_input, out_grad, precision=fast)
    direct = jnp.sum(inputs * vector, axis=-1)
    mix_state = decays * grad_match * step_size[None]
    grad_proj = jnp.einsum("usgh,ugn->sgn", mix_state, readout, precision=fast)
    grad_read = jnp.einsum("usgh,sgn->ugn", mix_state, input_proj, precision=fast)
    weights = mix_state * state_match[..., None]
    exclusive = jnp.cumsum(weights, axis=1) - weights
    paired = jnp.sum(exclusive * causal[:, :, None, None], axis=0)
    return (vector, direct, grad_proj, grad_read, paired)


def span_state(
    inputs_raw, out_raw, proj_raw, read_raw, step_size, decay_rate, state_in, grad_in, local
):
    vector, direct, grad_proj, grad_read, paired = local
    inputs = inputs_raw.astype(jnp.float32)
    out_grad = out_raw.astype(jnp.float32)
    input_proj = proj_raw.astype(jnp.float32)
    readout = read_raw.astype(jnp.float32)
    length = inputs.shape[0]
    position = jnp.arange(length)
    causal = (position[:, None] >= position[None, :]).astype(jnp.float32)
    strictly = (position[:, None] < position[None, :]).astype(jnp.float32)
    cumulative = jnp.cumsum(-decay_rate[None] * step_size, axis=0)
    totals = cumulative[-1]
    to_end = jnp.exp(totals[None] - cumulative)
    from_start = jnp.exp(cumulative)
    back_b = jnp.einsum("gnhp,sgn->sghp", grad_in, input_proj, precision=fast)
    vector = vector + to_end[..., None] * back_b
    grad_inputs = step_size[..., None] * vector
    tail_dot = jnp.sum(inputs * back_b, axis=-1)
    direct = direct + to_end * tail_dot
    scaled_x = (step_size * to_end)[..., None] * inputs
    grad_proj = grad_proj + jnp.einsum("sghp,gnhp->sgn", scaled_x, grad_in, precision=fast)
    scaled_y = from_start[..., None] * out_grad
    grad_read = grad_read + jnp.einsum("ughp,gnhp->ugn", scaled_y, state_in, precision=fast)
    read_state = jnp.einsum("ugn,gnhp->ughp", readout, state_in, precision=fast)
    from_init = from_start * jnp.sum(read_state * out_grad, axis=-1)
    suffixes = jnp.einsum("ut,ugh->tgh", causal, from_init, precision=fast)
    from_tail = to_end * step_size * tail_dot
    prefixes = jnp.einsum("st,sgh->tgh", strictly, from_tail, precision=fast)
    constant = jnp.exp(totals) * jnp.einsum("gnhp,gnhp->gh", grad_in, state_in, precision=fast)
    grad_log = paired + suffixes + prefixes + constant[None]
    grad_step = direct - decay_rate[None] * grad_log
    return (grad_inputs, grad_proj, grad_read, grad_step)


def combine(earlier, later):
    return (earlier[0] + later[0], jnp.exp(later[0])[:, None, :, None] * earlier[1] + later[1])


def span_prefix(log_sums, states, reverse):
    initial = (jnp.zeros_like(log_sums[0]), jnp.zeros_like(states[0]))

    def advance(carried, element):
        return (combine(carried, element), carried)

    return lax.scan(advance, initial, (log_sums, states), reverse=reverse)


def to_spans(
    inputs, out_grad, input_proj, readout, step_size, group_count, state_dim, head_dim, span_len
):
    span_count = inputs.shape[0] // span_len
    head_count = step_size.shape[1] // group_count
    return (
        inputs.reshape(span_count, span_len, group_count, head_count, head_dim),
        out_grad.reshape(span_count, span_len, group_count, head_count, head_dim),
        input_proj.reshape(span_count, span_len, group_count, state_dim),
        readout.reshape(span_count, span_len, group_count, state_dim),
        step_size.reshape(span_count, span_len, group_count, head_count),
    )


def over_spans(function, items):
    if jax.tree.leaves(items)[0].shape[0] == 1:
        return jax.tree.map(lambda a: a[None], function(jax.tree.map(lambda a: a[0], items)))
    return lax.map(function, items)


def body(inputs, input_proj, readout, step_size, decay_rate, out_grad):
    group_count = input_proj.shape[1] // D_STATE
    blocks = to_spans(
        inputs, out_grad, input_proj, readout, step_size, group_count, D_STATE, HEAD_DIM, SPAN
    )
    rate_rows = decay_rate.reshape(group_count, -1)
    totals, forward, backward = over_spans(lambda e: summarize(*e, rate_rows), blocks)
    if totals.shape[0] == 1:
        device_log, device_fwd, device_bwd = totals[0], forward[0], backward[0]
        log_before = log_after = jnp.zeros_like(totals)
        fwd_before = bwd_after = jnp.zeros_like(forward)
    else:
        (device_log, device_fwd), (log_before, fwd_before) = span_prefix(totals, forward, False)
        (ignored_log, device_bwd), (log_after, bwd_after) = span_prefix(totals, backward, True)
    local = over_spans(lambda e: span_local(*e, rate_rows), blocks)
    device_in, device_out = seq_scan(device_log, device_fwd, device_bwd, "seq")
    state_ins = fwd_before + jnp.exp(log_before)[:, :, None, :, None] * device_in[None]
    grad_ins = bwd_after + jnp.exp(log_after)[:, :, None, :, None] * device_out[None]
    gradients = over_spans(
        lambda e: span_state(*e[0], rate_rows, e[1], e[2], e[3]),
        (blocks, state_ins, grad_ins, local),
    )
    tokens = gradients[0].shape[0] * gradients[0].shape[1]
    grad_inputs, grad_proj, grad_read, grad_step = (g.reshape(tokens, -1) for g in gradients)
    regrouped = lax.all_to_all(grad_step, "tp", split_axis=0, concat_axis=1, tiled=True)
    return (
        grad_inputs.astype(jnp.bfloat16),
        grad_proj.astype(jnp.bfloat16),
        grad_read.astype(jnp.bfloat16),
        regrouped,
    )


def solution(mesh):
    in_specs = (
        P("seq", "tp"),
        P("seq", "tp"),
        P("seq", "tp"),
        P("seq", "tp"),
        P("tp"),
        P("seq", "tp"),
    )
    out_specs = (P("seq", "tp"), P("seq", "tp"), P("seq", "tp"), P(("seq", "tp"), None))
    return jax.shard_map(body, mesh=mesh, in_specs=in_specs, out_specs=out_specs, check_vma=False)
```

```python
import jax
import numpy as np
import jax.numpy as jnp
from jax import lax
from jax.sharding import PartitionSpec as P

HEAD_DIM = 64
D_STATE = 256
SPAN = 128


precise = lax.Precision.HIGHEST
fast = lax.Precision.HIGH


def prefix(part, axis, combine, identity, reverse):
    count = lax.axis_size(axis)
    place = lax.axis_index(axis)
    ahead = count - 1 - place if reverse else place
    gathered = jax.tree.map(lambda a: lax.all_gather(a, axis), part)
    state = jax.tree.map(lambda a, e: jnp.zeros_like(a) + jnp.asarray(e, a.dtype), part, identity)

    def one(turn, state):
        source = count - 1 - turn if reverse else turn
        return combine(
            state, jax.tree.map(lambda a: lax.dynamic_index_in_dim(a, source, 0, False), gathered)
        )

    return lax.fori_loop(0, ahead, one, state)


def seq_scan(device_log, device_fwd, device_bwd, axis):
    count = lax.axis_size(axis)
    place = lax.axis_index(axis)
    logs = device_log.reshape(-1)
    heads = logs.shape[0]
    stacked = jnp.stack([device_fwd, device_bwd]).transpose(0, 1, 3, 4, 2)
    shape = stacked.shape
    head_dim, state_dim = shape[3], shape[4]
    combos = 2 * heads
    if combos % count == 0:
        per = combos // count
        targets = np.arange(count)[:, None] * per + np.arange(per)[None, :]
        held = place * per + jnp.arange(per)
    else:
        per = 1
        targets = (np.arange(count) // (count // combos))[:, None]
        held = (place // (count // combos))[None]
    tiled = (count, per, head_dim // 8, 8, state_dim // 128, 128)
    flat = stacked.reshape(tiled).transpose(0, 1, 2, 4, 3, 5).reshape(count, -1, 128)
    body_rows = flat.shape[1]
    tags = jnp.broadcast_to(logs[targets % heads][..., None], (count, per, 128))
    chosen = lax.all_to_all(tags, axis, 0, 0, tiled=True)[:, :, 0]
    pieces = lax.all_to_all(flat, axis, 0, 0, tiled=True).reshape(count, per, -1)
    position = jnp.arange(count)
    low = jnp.minimum(position[:, None], position[None, :])
    high = jnp.maximum(position[:, None], position[None, :])
    between = ((position[None, None, :] > low[..., None]) & (position[None, None, :] < high[..., None]))
    exponent = jnp.einsum("ijm,mc->cij", between.astype(jnp.float32), chosen, precision=precise)
    before = (position[None, :] < position[:, None])
    after = (position[None, :] > position[:, None])
    mask = jnp.where((held < heads)[:, None, None], before[None], after[None])
    weights = jnp.where(mask, jnp.exp(exponent), 0.0)
    scanned = jnp.einsum("cij,jcx->icx", weights, pieces, precision=fast)
    back = lax.all_to_all(scanned.reshape(count, body_rows, 128), axis, 0, 0, tiled=True)
    back = back.reshape(count, per, head_dim // 8, state_dim // 128, 8, 128).transpose(0, 1, 2, 4, 3, 5)
    back = back.reshape(shape).transpose(0, 1, 4, 2, 3)
    return back[0], back[1]

def summarize(inputs, out_grad, input_proj, readout, step_size, decay_rate):
    cumulative = jnp.cumsum(-decay_rate[None] * step_size, axis=0)
    totals = cumulative[-1]
    to_end = jnp.exp(totals[None] - cumulative) * step_size
    forward = jnp.einsum(
        "qghp,qgn->gnhp",
        inputs.astype(jnp.float32) * to_end[..., None],
        input_proj.astype(jnp.float32),
        precision=fast,
    )
    from_start = jnp.exp(cumulative)
    backward = jnp.einsum(
        "qghp,qgn->gnhp",
        out_grad.astype(jnp.float32) * from_start[..., None],
        readout.astype(jnp.float32),
        precision=fast,
    )
    return (totals, forward, backward)


def span_local(inputs_raw, out_raw, proj_raw, read_raw, step_size, decay_rate):
    inputs = inputs_raw.astype(jnp.float32)
    out_grad = out_raw.astype(jnp.float32)
    input_proj = proj_raw.astype(jnp.float32)
    readout = read_raw.astype(jnp.float32)
    length = inputs.shape[0]
    position = jnp.arange(length)
    causal = (position[:, None] >= position[None, :]).astype(jnp.float32)
    cumulative = jnp.cumsum(-decay_rate[None] * step_size, axis=0)
    totals = cumulative[-1]
    spread = cumulative[:, None] - cumulative[None, :]
    decays = jnp.exp(jnp.minimum(spread, 0.0)) * causal[:, :, None, None]
    to_end = jnp.exp(totals[None] - cumulative)
    from_start = jnp.exp(cumulative)
    state_match = jnp.einsum("ugn,sgn->usg", read_raw, proj_raw, preferred_element_type=jnp.float32)
    grad_match = jnp.einsum(
        "ughp,sghp->usgh", out_raw, inputs_raw, preferred_element_type=jnp.float32
    )
    mix_input = decays * state_match[..., None]
    vector = jnp.einsum("usgh,ughp->sghp", mix_input, out_grad, precision=fast)
    direct = jnp.sum(inputs * vector, axis=-1)
    mix_state = decays * grad_match * step_size[None]
    grad_proj = jnp.einsum("usgh,ugn->sgn", mix_state, readout, precision=fast)
    grad_read = jnp.einsum("usgh,sgn->ugn", mix_state, input_proj, precision=fast)
    weights = mix_state * state_match[..., None]
    exclusive = jnp.cumsum(weights, axis=1) - weights
    paired = jnp.sum(exclusive * causal[:, :, None, None], axis=0)
    return (vector, direct, grad_proj, grad_read, paired)


def span_state(
    inputs_raw, out_raw, proj_raw, read_raw, step_size, decay_rate, state_in, grad_in, local
):
    vector, direct, grad_proj, grad_read, paired = local
    inputs = inputs_raw.astype(jnp.float32)
    out_grad = out_raw.astype(jnp.float32)
    input_proj = proj_raw.astype(jnp.float32)
    readout = read_raw.astype(jnp.float32)
    length = inputs.shape[0]
    position = jnp.arange(length)
    causal = (position[:, None] >= position[None, :]).astype(jnp.float32)
    strictly = (position[:, None] < position[None, :]).astype(jnp.float32)
    cumulative = jnp.cumsum(-decay_rate[None] * step_size, axis=0)
    totals = cumulative[-1]
    to_end = jnp.exp(totals[None] - cumulative)
    from_start = jnp.exp(cumulative)
    back_b = jnp.einsum("gnhp,sgn->sghp", grad_in, input_proj, precision=fast)
    vector = vector + to_end[..., None] * back_b
    grad_inputs = step_size[..., None] * vector
    tail_dot = jnp.sum(inputs * back_b, axis=-1)
    direct = direct + to_end * tail_dot
    scaled_x = (step_size * to_end)[..., None] * inputs
    grad_proj = grad_proj + jnp.einsum("sghp,gnhp->sgn", scaled_x, grad_in, precision=fast)
    scaled_y = from_start[..., None] * out_grad
    grad_read = grad_read + jnp.einsum("ughp,gnhp->ugn", scaled_y, state_in, precision=fast)
    read_state = jnp.einsum("ugn,gnhp->ughp", readout, state_in, precision=fast)
    from_init = from_start * jnp.sum(read_state * out_grad, axis=-1)
    suffixes = jnp.einsum("ut,ugh->tgh", causal, from_init, precision=fast)
    from_tail = to_end * step_size * tail_dot
    prefixes = jnp.einsum("st,sgh->tgh", strictly, from_tail, precision=fast)
    constant = jnp.exp(totals) * jnp.einsum("gnhp,gnhp->gh", grad_in, state_in, precision=fast)
    grad_log = paired + suffixes + prefixes + constant[None]
    grad_step = direct - decay_rate[None] * grad_log
    return (grad_inputs, grad_proj, grad_read, grad_step)


def combine(earlier, later):
    return (earlier[0] + later[0], jnp.exp(later[0])[:, None, :, None] * earlier[1] + later[1])


def span_prefix(log_sums, states, reverse):
    initial = (jnp.zeros_like(log_sums[0]), jnp.zeros_like(states[0]))

    def advance(carried, element):
        return (combine(carried, element), carried)

    return lax.scan(advance, initial, (log_sums, states), reverse=reverse)


def to_spans(
    inputs, out_grad, input_proj, readout, step_size, group_count, state_dim, head_dim, span_len
):
    span_count = inputs.shape[0] // span_len
    head_count = step_size.shape[1] // group_count
    return (
        inputs.reshape(span_count, span_len, group_count, head_count, head_dim),
        out_grad.reshape(span_count, span_len, group_count, head_count, head_dim),
        input_proj.reshape(span_count, span_len, group_count, state_dim),
        readout.reshape(span_count, span_len, group_count, state_dim),
        step_size.reshape(span_count, span_len, group_count, head_count),
    )


def over_spans(function, items):
    if jax.tree.leaves(items)[0].shape[0] == 1:
        return jax.tree.map(lambda a: a[None], function(jax.tree.map(lambda a: a[0], items)))
    return lax.map(function, items)


def body(inputs, input_proj, readout, step_size, decay_rate, out_grad):
    group_count = input_proj.shape[1] // D_STATE
    blocks = to_spans(
        inputs, out_grad, input_proj, readout, step_size, group_count, D_STATE, HEAD_DIM, SPAN
    )
    rate_rows = decay_rate.reshape(group_count, -1)
    totals, forward, backward = over_spans(lambda e: summarize(*e, rate_rows), blocks)
    if totals.shape[0] == 1:
        device_log, device_fwd, device_bwd = totals[0], forward[0], backward[0]
        log_before = log_after = jnp.zeros_like(totals)
        fwd_before = bwd_after = jnp.zeros_like(forward)
    else:
        (device_log, device_fwd), (log_before, fwd_before) = span_prefix(totals, forward, False)
        (ignored_log, device_bwd), (log_after, bwd_after) = span_prefix(totals, backward, True)
    local = over_spans(lambda e: span_local(*e, rate_rows), blocks)
    device_in, device_out = seq_scan(device_log, device_fwd, device_bwd, "seq")
    state_ins = fwd_before + jnp.exp(log_before)[:, :, None, :, None] * device_in[None]
    grad_ins = bwd_after + jnp.exp(log_after)[:, :, None, :, None] * device_out[None]
    gradients = over_spans(
        lambda e: span_state(*e[0], rate_rows, e[1], e[2], e[3]),
        (blocks, state_ins, grad_ins, local),
    )
    tokens = gradients[0].shape[0] * gradients[0].shape[1]
    grad_inputs, grad_proj, grad_read, grad_step = (g.reshape(tokens, -1) for g in gradients)
    regrouped = lax.all_to_all(grad_step, "tp", split_axis=0, concat_axis=1, tiled=True)
    return (
        grad_inputs.astype(jnp.bfloat16),
        grad_proj.astype(jnp.bfloat16),
        grad_read.astype(jnp.bfloat16),
        regrouped,
    )


def solution(mesh):
    in_specs = (
        P("seq", "tp"),
        P("seq", "tp"),
        P("seq", "tp"),
        P("seq", "tp"),
        P("tp"),
        P("seq", "tp"),
    )
    out_specs = (P("seq", "tp"), P("seq", "tp"), P("seq", "tp"), P(("seq", "tp"), None))
    return jax.shard_map(body, mesh=mesh, in_specs=in_specs, out_specs=out_specs, check_vma=False)
```

```python
import jax
import numpy as np
import jax.numpy as jnp
from jax import lax
from jax.sharding import PartitionSpec as P

HEAD_DIM = 64
D_STATE = 256
SPAN = 128


precise = lax.Precision.HIGHEST
fast = lax.Precision.HIGH


def prefix(part, axis, combine, identity, reverse):
    count = lax.axis_size(axis)
    place = lax.axis_index(axis)
    ahead = count - 1 - place if reverse else place
    gathered = jax.tree.map(lambda a: lax.all_gather(a, axis), part)
    state = jax.tree.map(lambda a, e: jnp.zeros_like(a) + jnp.asarray(e, a.dtype), part, identity)

    def one(turn, state):
        source = count - 1 - turn if reverse else turn
        return combine(
            state, jax.tree.map(lambda a: lax.dynamic_index_in_dim(a, source, 0, False), gathered)
        )

    return lax.fori_loop(0, ahead, one, state)


def seq_scan(device_log, device_fwd, device_bwd, axis):
    count = lax.axis_size(axis)
    place = lax.axis_index(axis)
    logs = device_log.reshape(-1)
    heads = logs.shape[0]
    stacked = jnp.stack([device_fwd, device_bwd]).transpose(0, 1, 3, 4, 2)
    shape = stacked.shape
    head_dim, state_dim = shape[3], shape[4]
    combos = 2 * heads
    if combos % count == 0:
        per = combos // count
        targets = np.arange(count)[:, None] * per + np.arange(per)[None, :]
        held = place * per + jnp.arange(per)
    else:
        per = 1
        targets = (np.arange(count) // (count // combos))[:, None]
        held = (place // (count // combos))[None]
    tiled = (count, per, head_dim // 8, 8, state_dim // 128, 128)
    flat = stacked.reshape(tiled).transpose(0, 1, 2, 4, 3, 5).reshape(count, -1, 128)
    body_rows = flat.shape[1]
    tags = jnp.repeat(logs[targets % heads], 8, axis=1)
    tags = jnp.broadcast_to(tags[..., None], (count, per * 8, 128))
    payload = jnp.concatenate([flat, tags], axis=1)
    pieces = lax.all_to_all(payload, axis, 0, 0, tiled=True)
    chosen = pieces[:, body_rows::8, 0]
    pieces = pieces[:, :body_rows, :].reshape(count, per, -1)
    position = jnp.arange(count)
    low = jnp.minimum(position[:, None], position[None, :])
    high = jnp.maximum(position[:, None], position[None, :])
    between = ((position[None, None, :] > low[..., None]) & (position[None, None, :] < high[..., None]))
    exponent = jnp.einsum("ijm,mc->cij", between.astype(jnp.float32), chosen, precision=precise)
    before = (position[None, :] < position[:, None])
    after = (position[None, :] > position[:, None])
    mask = jnp.where((held < heads)[:, None, None], before[None], after[None])
    weights = jnp.where(mask, jnp.exp(exponent), 0.0)
    scanned = jnp.einsum("cij,jcx->icx", weights, pieces, precision=fast)
    back = lax.all_to_all(scanned.reshape(count, body_rows, 128), axis, 0, 0, tiled=True)
    back = back.reshape(count, per, head_dim // 8, state_dim // 128, 8, 128).transpose(0, 1, 2, 4, 3, 5)
    back = back.reshape(shape).transpose(0, 1, 4, 2, 3)
    return back[0], back[1]

def summarize(inputs, out_grad, input_proj, readout, step_size, decay_rate):
    cumulative = jnp.cumsum(-decay_rate[None] * step_size, axis=0)
    totals = cumulative[-1]
    to_end = jnp.exp(totals[None] - cumulative) * step_size
    from_start = jnp.exp(cumulative)
    scaled = jnp.stack(
        [
            inputs.astype(jnp.float32) * to_end[..., None],
            out_grad.astype(jnp.float32) * from_start[..., None],
        ]
    )
    vectors = jnp.stack([input_proj.astype(jnp.float32), readout.astype(jnp.float32)])
    both = jnp.einsum("fqghp,fqgn->fgnhp", scaled, vectors, precision=fast)
    return (totals, both[0], both[1])


def span_local(inputs_raw, out_raw, proj_raw, read_raw, step_size, decay_rate):
    inputs = inputs_raw.astype(jnp.float32)
    out_grad = out_raw.astype(jnp.float32)
    input_proj = proj_raw.astype(jnp.float32)
    readout = read_raw.astype(jnp.float32)
    length = inputs.shape[0]
    position = jnp.arange(length)
    causal = (position[:, None] >= position[None, :]).astype(jnp.float32)
    cumulative = jnp.cumsum(-decay_rate[None] * step_size, axis=0)
    totals = cumulative[-1]
    spread = cumulative[:, None] - cumulative[None, :]
    decays = jnp.exp(jnp.minimum(spread, 0.0)) * causal[:, :, None, None]
    to_end = jnp.exp(totals[None] - cumulative)
    from_start = jnp.exp(cumulative)
    state_match = jnp.einsum("ugn,sgn->usg", read_raw, proj_raw, preferred_element_type=jnp.float32)
    grad_match = jnp.einsum(
        "ughp,sghp->usgh", out_raw, inputs_raw, preferred_element_type=jnp.float32
    )
    mix_input = decays * state_match[..., None]
    vector = jnp.einsum("usgh,ughp->sghp", mix_input, out_grad, precision=fast)
    direct = jnp.sum(inputs * vector, axis=-1)
    mix_state = decays * grad_match * step_size[None]
    grad_proj = jnp.einsum("usgh,ugn->sgn", mix_state, readout, precision=fast)
    grad_read = jnp.einsum("usgh,sgn->ugn", mix_state, input_proj, precision=fast)
    weights = mix_state * state_match[..., None]
    exclusive = jnp.cumsum(weights, axis=1) - weights
    paired = jnp.sum(exclusive * causal[:, :, None, None], axis=0)
    return (vector, direct, grad_proj, grad_read, paired)


def span_state(
    inputs_raw, out_raw, proj_raw, read_raw, step_size, decay_rate, state_in, grad_in, local
):
    vector, direct, grad_proj, grad_read, paired = local
    inputs = inputs_raw.astype(jnp.float32)
    out_grad = out_raw.astype(jnp.float32)
    input_proj = proj_raw.astype(jnp.float32)
    readout = read_raw.astype(jnp.float32)
    length = inputs.shape[0]
    position = jnp.arange(length)
    causal = (position[:, None] >= position[None, :]).astype(jnp.float32)
    strictly = (position[:, None] < position[None, :]).astype(jnp.float32)
    cumulative = jnp.cumsum(-decay_rate[None] * step_size, axis=0)
    totals = cumulative[-1]
    to_end = jnp.exp(totals[None] - cumulative)
    from_start = jnp.exp(cumulative)
    back_b = jnp.einsum("gnhp,sgn->sghp", grad_in, input_proj, precision=fast)
    vector = vector + to_end[..., None] * back_b
    grad_inputs = step_size[..., None] * vector
    tail_dot = jnp.sum(inputs * back_b, axis=-1)
    direct = direct + to_end * tail_dot
    scaled_x = (step_size * to_end)[..., None] * inputs
    grad_proj = grad_proj + jnp.einsum("sghp,gnhp->sgn", scaled_x, grad_in, precision=fast)
    scaled_y = from_start[..., None] * out_grad
    grad_read = grad_read + jnp.einsum("ughp,gnhp->ugn", scaled_y, state_in, precision=fast)
    read_state = jnp.einsum("ugn,gnhp->ughp", readout, state_in, precision=fast)
    from_init = from_start * jnp.sum(read_state * out_grad, axis=-1)
    suffixes = jnp.einsum("ut,ugh->tgh", causal, from_init, precision=fast)
    from_tail = to_end * step_size * tail_dot
    prefixes = jnp.einsum("st,sgh->tgh", strictly, from_tail, precision=fast)
    constant = jnp.exp(totals) * jnp.einsum("gnhp,gnhp->gh", grad_in, state_in, precision=fast)
    grad_log = paired + suffixes + prefixes + constant[None]
    grad_step = direct - decay_rate[None] * grad_log
    return (grad_inputs, grad_proj, grad_read, grad_step)


def combine(earlier, later):
    return (earlier[0] + later[0], jnp.exp(later[0])[:, None, :, None] * earlier[1] + later[1])


def span_prefix(log_sums, states, reverse):
    initial = (jnp.zeros_like(log_sums[0]), jnp.zeros_like(states[0]))

    def advance(carried, element):
        return (combine(carried, element), carried)

    return lax.scan(advance, initial, (log_sums, states), reverse=reverse)


def to_spans(
    inputs, out_grad, input_proj, readout, step_size, group_count, state_dim, head_dim, span_len
):
    span_count = inputs.shape[0] // span_len
    head_count = step_size.shape[1] // group_count
    return (
        inputs.reshape(span_count, span_len, group_count, head_count, head_dim),
        out_grad.reshape(span_count, span_len, group_count, head_count, head_dim),
        input_proj.reshape(span_count, span_len, group_count, state_dim),
        readout.reshape(span_count, span_len, group_count, state_dim),
        step_size.reshape(span_count, span_len, group_count, head_count),
    )


def over_spans(function, items):
    if jax.tree.leaves(items)[0].shape[0] == 1:
        return jax.tree.map(lambda a: a[None], function(jax.tree.map(lambda a: a[0], items)))
    return lax.map(function, items)


def body(inputs, input_proj, readout, step_size, decay_rate, out_grad):
    group_count = input_proj.shape[1] // D_STATE
    blocks = to_spans(
        inputs, out_grad, input_proj, readout, step_size, group_count, D_STATE, HEAD_DIM, SPAN
    )
    rate_rows = decay_rate.reshape(group_count, -1)
    totals, forward, backward = over_spans(lambda e: summarize(*e, rate_rows), blocks)
    if totals.shape[0] == 1:
        device_log, device_fwd, device_bwd = totals[0], forward[0], backward[0]
        log_before = log_after = jnp.zeros_like(totals)
        fwd_before = bwd_after = jnp.zeros_like(forward)
    else:
        (device_log, device_fwd), (log_before, fwd_before) = span_prefix(totals, forward, False)
        (ignored_log, device_bwd), (log_after, bwd_after) = span_prefix(totals, backward, True)
    local = over_spans(lambda e: span_local(*e, rate_rows), blocks)
    device_in, device_out = seq_scan(device_log, device_fwd, device_bwd, "seq")
    state_ins = fwd_before + jnp.exp(log_before)[:, :, None, :, None] * device_in[None]
    grad_ins = bwd_after + jnp.exp(log_after)[:, :, None, :, None] * device_out[None]
    gradients = over_spans(
        lambda e: span_state(*e[0], rate_rows, e[1], e[2], e[3]),
        (blocks, state_ins, grad_ins, local),
    )
    tokens = gradients[0].shape[0] * gradients[0].shape[1]
    grad_inputs, grad_proj, grad_read, grad_step = (g.reshape(tokens, -1) for g in gradients)
    regrouped = lax.all_to_all(grad_step, "tp", split_axis=0, concat_axis=1, tiled=True)
    return (
        grad_inputs.astype(jnp.bfloat16),
        grad_proj.astype(jnp.bfloat16),
        grad_read.astype(jnp.bfloat16),
        regrouped,
    )


def solution(mesh):
    in_specs = (
        P("seq", "tp"),
        P("seq", "tp"),
        P("seq", "tp"),
        P("seq", "tp"),
        P("tp"),
        P("seq", "tp"),
    )
    out_specs = (P("seq", "tp"), P("seq", "tp"), P("seq", "tp"), P(("seq", "tp"), None))
    return jax.shard_map(body, mesh=mesh, in_specs=in_specs, out_specs=out_specs, check_vma=False)
```

```python
import jax
import numpy as np
import jax.numpy as jnp
from jax import lax
from jax.sharding import PartitionSpec as P

HEAD_DIM = 64
D_STATE = 256
SPAN = 128


precise = lax.Precision.HIGHEST
fast = lax.Precision.HIGH


def prefix(part, axis, combine, identity, reverse):
    count = lax.axis_size(axis)
    place = lax.axis_index(axis)
    ahead = count - 1 - place if reverse else place
    gathered = jax.tree.map(lambda a: lax.all_gather(a, axis), part)
    state = jax.tree.map(lambda a, e: jnp.zeros_like(a) + jnp.asarray(e, a.dtype), part, identity)

    def one(turn, state):
        source = count - 1 - turn if reverse else turn
        return combine(
            state, jax.tree.map(lambda a: lax.dynamic_index_in_dim(a, source, 0, False), gathered)
        )

    return lax.fori_loop(0, ahead, one, state)


def seq_scan(device_log, device_fwd, device_bwd, axis):
    count = lax.axis_size(axis)
    place = lax.axis_index(axis)
    logs = device_log.reshape(-1)
    heads = logs.shape[0]
    stacked = jnp.stack([device_fwd, device_bwd]).transpose(0, 1, 3, 4, 2)
    shape = stacked.shape
    head_dim, state_dim = shape[3], shape[4]
    combos = 2 * heads
    if combos % count == 0:
        per = combos // count
        targets = np.arange(count)[:, None] * per + np.arange(per)[None, :]
        held = place * per + jnp.arange(per)
    else:
        per = 1
        targets = (np.arange(count) // (count // combos))[:, None]
        held = (place // (count // combos))[None]
    tiled = (count, per, head_dim // 8, 8, state_dim // 128, 128)
    flat = stacked.reshape(tiled).transpose(0, 1, 2, 4, 3, 5).reshape(count, -1, 128)
    body_rows = flat.shape[1]
    tags = jnp.repeat(jnp.stack([logs[i % heads] for i in targets.reshape(-1)]).reshape(targets.shape), 8, axis=1)
    tags = jnp.broadcast_to(tags[..., None], (count, per * 8, 128))
    payload = jnp.concatenate([flat, tags], axis=1)
    pieces = lax.all_to_all(payload, axis, 0, 0, tiled=True)
    chosen = pieces[:, body_rows::8, 0]
    pieces = pieces[:, :body_rows, :].reshape(count, per, -1)
    position = jnp.arange(count)
    low = jnp.minimum(position[:, None], position[None, :])
    high = jnp.maximum(position[:, None], position[None, :])
    between = ((position[None, None, :] > low[..., None]) & (position[None, None, :] < high[..., None]))
    exponent = jnp.einsum("ijm,mc->cij", between.astype(jnp.float32), chosen, precision=precise)
    before = (position[None, :] < position[:, None])
    after = (position[None, :] > position[:, None])
    mask = jnp.where((held < heads)[:, None, None], before[None], after[None])
    weights = jnp.where(mask, jnp.exp(exponent), 0.0)
    scanned = jnp.einsum("cij,jcx->icx", weights, pieces, precision=fast)
    back = lax.all_to_all(scanned.reshape(count, body_rows, 128), axis, 0, 0, tiled=True)
    back = back.reshape(count, per, head_dim // 8, state_dim // 128, 8, 128).transpose(0, 1, 2, 4, 3, 5)
    back = back.reshape(shape).transpose(0, 1, 4, 2, 3)
    return back[0], back[1]

def summarize(inputs, out_grad, input_proj, readout, step_size, decay_rate):
    cumulative = jnp.cumsum(-decay_rate[None] * step_size, axis=0)
    totals = cumulative[-1]
    to_end = jnp.exp(totals[None] - cumulative) * step_size
    from_start = jnp.exp(cumulative)
    scaled = jnp.stack(
        [
            inputs.astype(jnp.float32) * to_end[..., None],
            out_grad.astype(jnp.float32) * from_start[..., None],
        ]
    )
    vectors = jnp.stack([input_proj.astype(jnp.float32), readout.astype(jnp.float32)])
    both = jnp.einsum("fqghp,fqgn->fgnhp", scaled, vectors, precision=fast)
    return (totals, both[0], both[1])


def span_local(inputs_raw, out_raw, proj_raw, read_raw, step_size, decay_rate):
    inputs = inputs_raw.astype(jnp.float32)
    out_grad = out_raw.astype(jnp.float32)
    input_proj = proj_raw.astype(jnp.float32)
    readout = read_raw.astype(jnp.float32)
    length = inputs.shape[0]
    position = jnp.arange(length)
    causal = (position[:, None] >= position[None, :]).astype(jnp.float32)
    cumulative = jnp.cumsum(-decay_rate[None] * step_size, axis=0)
    totals = cumulative[-1]
    spread = cumulative[:, None] - cumulative[None, :]
    decays = jnp.exp(jnp.minimum(spread, 0.0)) * causal[:, :, None, None]
    to_end = jnp.exp(totals[None] - cumulative)
    from_start = jnp.exp(cumulative)
    state_match = jnp.einsum("ugn,sgn->usg", read_raw, proj_raw, preferred_element_type=jnp.float32)
    grad_match = jnp.einsum(
        "ughp,sghp->usgh", out_raw, inputs_raw, preferred_element_type=jnp.float32
    )
    mix_input = decays * state_match[..., None]
    vector = jnp.einsum("usgh,ughp->sghp", mix_input, out_grad, precision=fast)
    direct = jnp.sum(inputs * vector, axis=-1)
    mix_state = decays * grad_match * step_size[None]
    grad_proj = jnp.einsum("usgh,ugn->sgn", mix_state, readout, precision=fast)
    grad_read = jnp.einsum("usgh,sgn->ugn", mix_state, input_proj, precision=fast)
    weights = mix_state * state_match[..., None]
    exclusive = jnp.cumsum(weights, axis=1) - weights
    paired = jnp.sum(exclusive * causal[:, :, None, None], axis=0)
    return (vector, direct, grad_proj, grad_read, paired)


def span_state(
    inputs_raw, out_raw, proj_raw, read_raw, step_size, decay_rate, state_in, grad_in, local
):
    vector, direct, grad_proj, grad_read, paired = local
    inputs = inputs_raw.astype(jnp.float32)
    out_grad = out_raw.astype(jnp.float32)
    input_proj = proj_raw.astype(jnp.float32)
    readout = read_raw.astype(jnp.float32)
    length = inputs.shape[0]
    position = jnp.arange(length)
    causal = (position[:, None] >= position[None, :]).astype(jnp.float32)
    strictly = (position[:, None] < position[None, :]).astype(jnp.float32)
    cumulative = jnp.cumsum(-decay_rate[None] * step_size, axis=0)
    totals = cumulative[-1]
    to_end = jnp.exp(totals[None] - cumulative)
    from_start = jnp.exp(cumulative)
    back_b = jnp.einsum("gnhp,sgn->sghp", grad_in, input_proj, precision=fast)
    vector = vector + to_end[..., None] * back_b
    grad_inputs = step_size[..., None] * vector
    tail_dot = jnp.sum(inputs * back_b, axis=-1)
    direct = direct + to_end * tail_dot
    scaled_x = (step_size * to_end)[..., None] * inputs
    grad_proj = grad_proj + jnp.einsum("sghp,gnhp->sgn", scaled_x, grad_in, precision=fast)
    scaled_y = from_start[..., None] * out_grad
    grad_read = grad_read + jnp.einsum("ughp,gnhp->ugn", scaled_y, state_in, precision=fast)
    read_state = jnp.einsum("ugn,gnhp->ughp", readout, state_in, precision=fast)
    from_init = from_start * jnp.sum(read_state * out_grad, axis=-1)
    suffixes = jnp.einsum("ut,ugh->tgh", causal, from_init, precision=fast)
    from_tail = to_end * step_size * tail_dot
    prefixes = jnp.einsum("st,sgh->tgh", strictly, from_tail, precision=fast)
    constant = jnp.exp(totals) * jnp.einsum("gnhp,gnhp->gh", grad_in, state_in, precision=fast)
    grad_log = paired + suffixes + prefixes + constant[None]
    grad_step = direct - decay_rate[None] * grad_log
    return (grad_inputs, grad_proj, grad_read, grad_step)


def combine(earlier, later):
    return (earlier[0] + later[0], jnp.exp(later[0])[:, None, :, None] * earlier[1] + later[1])


def span_prefix(log_sums, states, reverse):
    initial = (jnp.zeros_like(log_sums[0]), jnp.zeros_like(states[0]))

    def advance(carried, element):
        return (combine(carried, element), carried)

    return lax.scan(advance, initial, (log_sums, states), reverse=reverse)


def to_spans(
    inputs, out_grad, input_proj, readout, step_size, group_count, state_dim, head_dim, span_len
):
    span_count = inputs.shape[0] // span_len
    head_count = step_size.shape[1] // group_count
    return (
        inputs.reshape(span_count, span_len, group_count, head_count, head_dim),
        out_grad.reshape(span_count, span_len, group_count, head_count, head_dim),
        input_proj.reshape(span_count, span_len, group_count, state_dim),
        readout.reshape(span_count, span_len, group_count, state_dim),
        step_size.reshape(span_count, span_len, group_count, head_count),
    )


def over_spans(function, items):
    if jax.tree.leaves(items)[0].shape[0] == 1:
        return jax.tree.map(lambda a: a[None], function(jax.tree.map(lambda a: a[0], items)))
    return lax.map(function, items)


def body(inputs, input_proj, readout, step_size, decay_rate, out_grad):
    group_count = input_proj.shape[1] // D_STATE
    blocks = to_spans(
        inputs, out_grad, input_proj, readout, step_size, group_count, D_STATE, HEAD_DIM, SPAN
    )
    rate_rows = decay_rate.reshape(group_count, -1)
    totals, forward, backward = over_spans(lambda e: summarize(*e, rate_rows), blocks)
    if totals.shape[0] == 1:
        device_log, device_fwd, device_bwd = totals[0], forward[0], backward[0]
        log_before = log_after = jnp.zeros_like(totals)
        fwd_before = bwd_after = jnp.zeros_like(forward)
    else:
        (device_log, device_fwd), (log_before, fwd_before) = span_prefix(totals, forward, False)
        (ignored_log, device_bwd), (log_after, bwd_after) = span_prefix(totals, backward, True)
    local = over_spans(lambda e: span_local(*e, rate_rows), blocks)
    device_in, device_out = seq_scan(device_log, device_fwd, device_bwd, "seq")
    state_ins = fwd_before + jnp.exp(log_before)[:, :, None, :, None] * device_in[None]
    grad_ins = bwd_after + jnp.exp(log_after)[:, :, None, :, None] * device_out[None]
    gradients = over_spans(
        lambda e: span_state(*e[0], rate_rows, e[1], e[2], e[3]),
        (blocks, state_ins, grad_ins, local),
    )
    tokens = gradients[0].shape[0] * gradients[0].shape[1]
    grad_inputs, grad_proj, grad_read, grad_step = (g.reshape(tokens, -1) for g in gradients)
    regrouped = lax.all_to_all(grad_step, "tp", split_axis=0, concat_axis=1, tiled=True)
    return (
        grad_inputs.astype(jnp.bfloat16),
        grad_proj.astype(jnp.bfloat16),
        grad_read.astype(jnp.bfloat16),
        regrouped,
    )


def solution(mesh):
    in_specs = (
        P("seq", "tp"),
        P("seq", "tp"),
        P("seq", "tp"),
        P("seq", "tp"),
        P("tp"),
        P("seq", "tp"),
    )
    out_specs = (P("seq", "tp"), P("seq", "tp"), P("seq", "tp"), P(("seq", "tp"), None))
    return jax.shard_map(body, mesh=mesh, in_specs=in_specs, out_specs=out_specs, check_vma=False)
```

```python
import jax
import numpy as np
import jax.numpy as jnp
from jax import lax
from jax.sharding import PartitionSpec as P

HEAD_DIM = 64
D_STATE = 256
SPAN = 128


precise = lax.Precision.HIGHEST
fast = lax.Precision.HIGH


def prefix(part, axis, combine, identity, reverse):
    count = lax.axis_size(axis)
    place = lax.axis_index(axis)
    ahead = count - 1 - place if reverse else place
    gathered = jax.tree.map(lambda a: lax.all_gather(a, axis), part)
    state = jax.tree.map(lambda a, e: jnp.zeros_like(a) + jnp.asarray(e, a.dtype), part, identity)

    def one(turn, state):
        source = count - 1 - turn if reverse else turn
        return combine(
            state, jax.tree.map(lambda a: lax.dynamic_index_in_dim(a, source, 0, False), gathered)
        )

    return lax.fori_loop(0, ahead, one, state)


def seq_scan(device_log, device_fwd, device_bwd, axis):
    count = lax.axis_size(axis)
    place = lax.axis_index(axis)
    logs = device_log.reshape(-1)
    heads = logs.shape[0]
    stacked = jnp.stack([device_fwd, device_bwd]).transpose(0, 1, 3, 4, 2)
    shape = stacked.shape
    head_dim, state_dim = shape[3], shape[4]
    combos = 2 * heads
    if combos % count == 0:
        per = combos // count
        targets = np.arange(count)[:, None] * per + np.arange(per)[None, :]
        held = place * per + jnp.arange(per)
    else:
        per = 1
        targets = (np.arange(count) // (count // combos))[:, None]
        held = (place // (count // combos))[None]
    tiled = (count, per, head_dim // 8, 8, state_dim // 128, 128)
    flat = stacked.reshape(tiled).transpose(0, 1, 2, 4, 3, 5).reshape(count, -1, 128)
    body_rows = flat.shape[1]
    tags = jnp.repeat(logs[targets % heads], 8, axis=1)
    tags = jnp.broadcast_to(tags[..., None], (count, per * 8, 128))
    payload = jnp.concatenate([flat, tags], axis=1)
    pieces = lax.all_to_all(payload, axis, 0, 0, tiled=True)
    chosen = pieces[:, body_rows::8, 0]
    pieces = pieces[:, :body_rows, :].reshape(count, per, body_rows // per, 128)
    position = jnp.arange(count)
    low = jnp.minimum(position[:, None], position[None, :])
    high = jnp.maximum(position[:, None], position[None, :])
    between = ((position[None, None, :] > low[..., None]) & (position[None, None, :] < high[..., None]))
    exponent = jnp.einsum("ijm,mc->cij", between.astype(jnp.float32), chosen, precision=precise)
    before = (position[None, :] < position[:, None])
    after = (position[None, :] > position[:, None])
    mask = jnp.where((held < heads)[:, None, None], before[None], after[None])
    weights = jnp.where(mask, jnp.exp(exponent), 0.0)
    scanned = jnp.sum(weights.transpose(1, 2, 0)[:, :, :, None, None] * pieces[None], axis=1)
    back = lax.all_to_all(scanned.reshape(count, body_rows, 128), axis, 0, 0, tiled=True)
    back = back.reshape(count, per, head_dim // 8, state_dim // 128, 8, 128).transpose(0, 1, 2, 4, 3, 5)
    back = back.reshape(shape).transpose(0, 1, 4, 2, 3)
    return back[0], back[1]

def summarize(inputs, out_grad, input_proj, readout, step_size, decay_rate):
    cumulative = jnp.cumsum(-decay_rate[None] * step_size, axis=0)
    totals = cumulative[-1]
    to_end = jnp.exp(totals[None] - cumulative) * step_size
    from_start = jnp.exp(cumulative)
    scaled = jnp.stack(
        [
            inputs.astype(jnp.float32) * to_end[..., None],
            out_grad.astype(jnp.float32) * from_start[..., None],
        ]
    )
    vectors = jnp.stack([input_proj.astype(jnp.float32), readout.astype(jnp.float32)])
    both = jnp.einsum("fqghp,fqgn->fgnhp", scaled, vectors, precision=fast)
    return (totals, both[0], both[1])


def span_local(inputs_raw, out_raw, proj_raw, read_raw, step_size, decay_rate):
    inputs = inputs_raw.astype(jnp.float32)
    out_grad = out_raw.astype(jnp.float32)
    input_proj = proj_raw.astype(jnp.float32)
    readout = read_raw.astype(jnp.float32)
    length = inputs.shape[0]
    position = jnp.arange(length)
    causal = (position[:, None] >= position[None, :]).astype(jnp.float32)
    cumulative = jnp.cumsum(-decay_rate[None] * step_size, axis=0)
    totals = cumulative[-1]
    spread = cumulative[:, None] - cumulative[None, :]
    decays = jnp.exp(jnp.minimum(spread, 0.0)) * causal[:, :, None, None]
    to_end = jnp.exp(totals[None] - cumulative)
    from_start = jnp.exp(cumulative)
    state_match = jnp.einsum("ugn,sgn->usg", read_raw, proj_raw, preferred_element_type=jnp.float32)
    grad_match = jnp.einsum(
        "ughp,sghp->usgh", out_raw, inputs_raw, preferred_element_type=jnp.float32
    )
    mix_input = decays * state_match[..., None]
    vector = jnp.einsum("usgh,ughp->sghp", mix_input, out_grad, precision=fast)
    direct = jnp.sum(inputs * vector, axis=-1)
    mix_state = decays * grad_match * step_size[None]
    grad_proj = jnp.einsum("usgh,ugn->sgn", mix_state, readout, precision=fast)
    grad_read = jnp.einsum("usgh,sgn->ugn", mix_state, input_proj, precision=fast)
    weights = mix_state * state_match[..., None]
    exclusive = jnp.cumsum(weights, axis=1) - weights
    paired = jnp.sum(exclusive * causal[:, :, None, None], axis=0)
    return (vector, direct, grad_proj, grad_read, paired)


def span_state(
    inputs_raw, out_raw, proj_raw, read_raw, step_size, decay_rate, state_in, grad_in, local
):
    vector, direct, grad_proj, grad_read, paired = local
    inputs = inputs_raw.astype(jnp.float32)
    out_grad = out_raw.astype(jnp.float32)
    input_proj = proj_raw.astype(jnp.float32)
    readout = read_raw.astype(jnp.float32)
    length = inputs.shape[0]
    position = jnp.arange(length)
    causal = (position[:, None] >= position[None, :]).astype(jnp.float32)
    strictly = (position[:, None] < position[None, :]).astype(jnp.float32)
    cumulative = jnp.cumsum(-decay_rate[None] * step_size, axis=0)
    totals = cumulative[-1]
    to_end = jnp.exp(totals[None] - cumulative)
    from_start = jnp.exp(cumulative)
    back_b = jnp.einsum("gnhp,sgn->sghp", grad_in, input_proj, precision=fast)
    vector = vector + to_end[..., None] * back_b
    grad_inputs = step_size[..., None] * vector
    tail_dot = jnp.sum(inputs * back_b, axis=-1)
    direct = direct + to_end * tail_dot
    scaled_x = (step_size * to_end)[..., None] * inputs
    grad_proj = grad_proj + jnp.einsum("sghp,gnhp->sgn", scaled_x, grad_in, precision=fast)
    scaled_y = from_start[..., None] * out_grad
    grad_read = grad_read + jnp.einsum("ughp,gnhp->ugn", scaled_y, state_in, precision=fast)
    read_state = jnp.einsum("ugn,gnhp->ughp", readout, state_in, precision=fast)
    from_init = from_start * jnp.sum(read_state * out_grad, axis=-1)
    suffixes = jnp.einsum("ut,ugh->tgh", causal, from_init, precision=fast)
    from_tail = to_end * step_size * tail_dot
    prefixes = jnp.einsum("st,sgh->tgh", strictly, from_tail, precision=fast)
    constant = jnp.exp(totals) * jnp.einsum("gnhp,gnhp->gh", grad_in, state_in, precision=fast)
    grad_log = paired + suffixes + prefixes + constant[None]
    grad_step = direct - decay_rate[None] * grad_log
    return (grad_inputs, grad_proj, grad_read, grad_step)


def combine(earlier, later):
    return (earlier[0] + later[0], jnp.exp(later[0])[:, None, :, None] * earlier[1] + later[1])


def span_prefix(log_sums, states, reverse):
    initial = (jnp.zeros_like(log_sums[0]), jnp.zeros_like(states[0]))

    def advance(carried, element):
        return (combine(carried, element), carried)

    return lax.scan(advance, initial, (log_sums, states), reverse=reverse)


def to_spans(
    inputs, out_grad, input_proj, readout, step_size, group_count, state_dim, head_dim, span_len
):
    span_count = inputs.shape[0] // span_len
    head_count = step_size.shape[1] // group_count
    return (
        inputs.reshape(span_count, span_len, group_count, head_count, head_dim),
        out_grad.reshape(span_count, span_len, group_count, head_count, head_dim),
        input_proj.reshape(span_count, span_len, group_count, state_dim),
        readout.reshape(span_count, span_len, group_count, state_dim),
        step_size.reshape(span_count, span_len, group_count, head_count),
    )


def over_spans(function, items):
    if jax.tree.leaves(items)[0].shape[0] == 1:
        return jax.tree.map(lambda a: a[None], function(jax.tree.map(lambda a: a[0], items)))
    return lax.map(function, items)


def body(inputs, input_proj, readout, step_size, decay_rate, out_grad):
    group_count = input_proj.shape[1] // D_STATE
    blocks = to_spans(
        inputs, out_grad, input_proj, readout, step_size, group_count, D_STATE, HEAD_DIM, SPAN
    )
    rate_rows = decay_rate.reshape(group_count, -1)
    totals, forward, backward = over_spans(lambda e: summarize(*e, rate_rows), blocks)
    if totals.shape[0] == 1:
        device_log, device_fwd, device_bwd = totals[0], forward[0], backward[0]
        log_before = log_after = jnp.zeros_like(totals)
        fwd_before = bwd_after = jnp.zeros_like(forward)
    else:
        (device_log, device_fwd), (log_before, fwd_before) = span_prefix(totals, forward, False)
        (ignored_log, device_bwd), (log_after, bwd_after) = span_prefix(totals, backward, True)
    local = over_spans(lambda e: span_local(*e, rate_rows), blocks)
    device_in, device_out = seq_scan(device_log, device_fwd, device_bwd, "seq")
    state_ins = fwd_before + jnp.exp(log_before)[:, :, None, :, None] * device_in[None]
    grad_ins = bwd_after + jnp.exp(log_after)[:, :, None, :, None] * device_out[None]
    gradients = over_spans(
        lambda e: span_state(*e[0], rate_rows, e[1], e[2], e[3]),
        (blocks, state_ins, grad_ins, local),
    )
    tokens = gradients[0].shape[0] * gradients[0].shape[1]
    grad_inputs, grad_proj, grad_read, grad_step = (g.reshape(tokens, -1) for g in gradients)
    regrouped = lax.all_to_all(grad_step, "tp", split_axis=0, concat_axis=1, tiled=True)
    return (
        grad_inputs.astype(jnp.bfloat16),
        grad_proj.astype(jnp.bfloat16),
        grad_read.astype(jnp.bfloat16),
        regrouped,
    )


def solution(mesh):
    in_specs = (
        P("seq", "tp"),
        P("seq", "tp"),
        P("seq", "tp"),
        P("seq", "tp"),
        P("tp"),
        P("seq", "tp"),
    )
    out_specs = (P("seq", "tp"), P("seq", "tp"), P("seq", "tp"), P(("seq", "tp"), None))
    return jax.shard_map(body, mesh=mesh, in_specs=in_specs, out_specs=out_specs, check_vma=False)
```

```python
import jax
import numpy as np
import jax.numpy as jnp
from jax import lax
from jax.sharding import PartitionSpec as P

HEAD_DIM = 64
D_STATE = 256
SPAN = 128


precise = lax.Precision.HIGHEST
fast = lax.Precision.HIGH


def prefix(part, axis, combine, identity, reverse):
    count = lax.axis_size(axis)
    place = lax.axis_index(axis)
    ahead = count - 1 - place if reverse else place
    gathered = jax.tree.map(lambda a: lax.all_gather(a, axis), part)
    state = jax.tree.map(lambda a, e: jnp.zeros_like(a) + jnp.asarray(e, a.dtype), part, identity)

    def one(turn, state):
        source = count - 1 - turn if reverse else turn
        return combine(
            state, jax.tree.map(lambda a: lax.dynamic_index_in_dim(a, source, 0, False), gathered)
        )

    return lax.fori_loop(0, ahead, one, state)


def seq_scan(device_log, device_fwd, device_bwd, axis):
    count = lax.axis_size(axis)
    place = lax.axis_index(axis)
    logs = device_log.reshape(-1)
    heads = logs.shape[0]
    stacked = jnp.stack([device_fwd, device_bwd]).transpose(0, 1, 3, 4, 2)
    shape = stacked.shape
    head_dim, state_dim = shape[3], shape[4]
    combos = 2 * heads
    if combos % count == 0:
        per = combos // count
        targets = np.arange(count)[:, None] * per + np.arange(per)[None, :]
        held = place * per + jnp.arange(per)
    else:
        per = 1
        targets = (np.arange(count) // (count // combos))[:, None]
        held = (place // (count // combos))[None]
    tiled = (count, per, head_dim // 8, 8, state_dim // 128, 128)
    flat = stacked.reshape(tiled).transpose(0, 1, 2, 4, 3, 5).reshape(count, -1, 128)
    body_rows = flat.shape[1]
    owned = targets % heads
    if per == 1 and np.array_equal(owned[:, 0], np.arange(count) % heads):
        chosen_logs = jnp.tile(logs, count // heads)[:, None]
    else:
        chosen_logs = logs[owned]
    tags = jnp.repeat(chosen_logs, 8, axis=1)
    tags = jnp.broadcast_to(tags[..., None], (count, per * 8, 128))
    payload = jnp.concatenate([flat, tags], axis=1)
    pieces = lax.all_to_all(payload, axis, 0, 0, tiled=True)
    chosen = pieces[:, body_rows::8, 0]
    pieces = pieces[:, :body_rows, :].reshape(count, per, -1)
    position = jnp.arange(count)
    low = jnp.minimum(position[:, None], position[None, :])
    high = jnp.maximum(position[:, None], position[None, :])
    between = ((position[None, None, :] > low[..., None]) & (position[None, None, :] < high[..., None]))
    exponent = jnp.einsum("ijm,mc->cij", between.astype(jnp.float32), chosen, precision=precise)
    before = (position[None, :] < position[:, None])
    after = (position[None, :] > position[:, None])
    mask = jnp.where((held < heads)[:, None, None], before[None], after[None])
    weights = jnp.where(mask, jnp.exp(exponent), 0.0)
    scanned = jnp.einsum("cij,jcx->icx", weights, pieces, precision=fast)
    back = lax.all_to_all(scanned.reshape(count, body_rows, 128), axis, 0, 0, tiled=True)
    back = back.reshape(count, per, head_dim // 8, state_dim // 128, 8, 128).transpose(0, 1, 2, 4, 3, 5)
    back = back.reshape(shape).transpose(0, 1, 4, 2, 3)
    return back[0], back[1]

def summarize(inputs, out_grad, input_proj, readout, step_size, decay_rate):
    cumulative = jnp.cumsum(-decay_rate[None] * step_size, axis=0)
    totals = cumulative[-1]
    to_end = jnp.exp(totals[None] - cumulative) * step_size
    from_start = jnp.exp(cumulative)
    scaled = jnp.stack(
        [
            inputs.astype(jnp.float32) * to_end[..., None],
            out_grad.astype(jnp.float32) * from_start[..., None],
        ]
    )
    vectors = jnp.stack([input_proj.astype(jnp.float32), readout.astype(jnp.float32)])
    both = jnp.einsum("fqghp,fqgn->fgnhp", scaled, vectors, precision=fast)
    return (totals, both[0], both[1])


def span_local(inputs_raw, out_raw, proj_raw, read_raw, step_size, decay_rate):
    inputs = inputs_raw.astype(jnp.float32)
    out_grad = out_raw.astype(jnp.float32)
    input_proj = proj_raw.astype(jnp.float32)
    readout = read_raw.astype(jnp.float32)
    length = inputs.shape[0]
    position = jnp.arange(length)
    causal = (position[:, None] >= position[None, :]).astype(jnp.float32)
    cumulative = jnp.cumsum(-decay_rate[None] * step_size, axis=0)
    totals = cumulative[-1]
    spread = cumulative[:, None] - cumulative[None, :]
    decays = jnp.exp(jnp.minimum(spread, 0.0)) * causal[:, :, None, None]
    to_end = jnp.exp(totals[None] - cumulative)
    from_start = jnp.exp(cumulative)
    state_match = jnp.einsum("ugn,sgn->usg", read_raw, proj_raw, preferred_element_type=jnp.float32)
    grad_match = jnp.einsum(
        "ughp,sghp->usgh", out_raw, inputs_raw, preferred_element_type=jnp.float32
    )
    mix_input = decays * state_match[..., None]
    vector = jnp.einsum("usgh,ughp->sghp", mix_input, out_grad, precision=fast)
    direct = jnp.sum(inputs * vector, axis=-1)
    mix_state = decays * grad_match * step_size[None]
    grad_proj = jnp.einsum("usgh,ugn->sgn", mix_state, readout, precision=fast)
    grad_read = jnp.einsum("usgh,sgn->ugn", mix_state, input_proj, precision=fast)
    weights = mix_state * state_match[..., None]
    exclusive = jnp.cumsum(weights, axis=1) - weights
    paired = jnp.sum(exclusive * causal[:, :, None, None], axis=0)
    return (vector, direct, grad_proj, grad_read, paired)


def span_state(
    inputs_raw, out_raw, proj_raw, read_raw, step_size, decay_rate, state_in, grad_in, local
):
    vector, direct, grad_proj, grad_read, paired = local
    inputs = inputs_raw.astype(jnp.float32)
    out_grad = out_raw.astype(jnp.float32)
    input_proj = proj_raw.astype(jnp.float32)
    readout = read_raw.astype(jnp.float32)
    length = inputs.shape[0]
    position = jnp.arange(length)
    causal = (position[:, None] >= position[None, :]).astype(jnp.float32)
    strictly = (position[:, None] < position[None, :]).astype(jnp.float32)
    cumulative = jnp.cumsum(-decay_rate[None] * step_size, axis=0)
    totals = cumulative[-1]
    to_end = jnp.exp(totals[None] - cumulative)
    from_start = jnp.exp(cumulative)
    back_b = jnp.einsum("gnhp,sgn->sghp", grad_in, input_proj, precision=fast)
    vector = vector + to_end[..., None] * back_b
    grad_inputs = step_size[..., None] * vector
    tail_dot = jnp.sum(inputs * back_b, axis=-1)
    direct = direct + to_end * tail_dot
    scaled_x = (step_size * to_end)[..., None] * inputs
    grad_proj = grad_proj + jnp.einsum("sghp,gnhp->sgn", scaled_x, grad_in, precision=fast)
    scaled_y = from_start[..., None] * out_grad
    grad_read = grad_read + jnp.einsum("ughp,gnhp->ugn", scaled_y, state_in, precision=fast)
    read_state = jnp.einsum("ugn,gnhp->ughp", readout, state_in, precision=fast)
    from_init = from_start * jnp.sum(read_state * out_grad, axis=-1)
    suffixes = jnp.einsum("ut,ugh->tgh", causal, from_init, precision=fast)
    from_tail = to_end * step_size * tail_dot
    prefixes = jnp.einsum("st,sgh->tgh", strictly, from_tail, precision=fast)
    constant = jnp.exp(totals) * jnp.einsum("gnhp,gnhp->gh", grad_in, state_in, precision=fast)
    grad_log = paired + suffixes + prefixes + constant[None]
    grad_step = direct - decay_rate[None] * grad_log
    return (grad_inputs, grad_proj, grad_read, grad_step)


def combine(earlier, later):
    return (earlier[0] + later[0], jnp.exp(later[0])[:, None, :, None] * earlier[1] + later[1])


def span_prefix(log_sums, states, reverse):
    initial = (jnp.zeros_like(log_sums[0]), jnp.zeros_like(states[0]))

    def advance(carried, element):
        return (combine(carried, element), carried)

    return lax.scan(advance, initial, (log_sums, states), reverse=reverse)


def to_spans(
    inputs, out_grad, input_proj, readout, step_size, group_count, state_dim, head_dim, span_len
):
    span_count = inputs.shape[0] // span_len
    head_count = step_size.shape[1] // group_count
    return (
        inputs.reshape(span_count, span_len, group_count, head_count, head_dim),
        out_grad.reshape(span_count, span_len, group_count, head_count, head_dim),
        input_proj.reshape(span_count, span_len, group_count, state_dim),
        readout.reshape(span_count, span_len, group_count, state_dim),
        step_size.reshape(span_count, span_len, group_count, head_count),
    )


def over_spans(function, items):
    if jax.tree.leaves(items)[0].shape[0] == 1:
        return jax.tree.map(lambda a: a[None], function(jax.tree.map(lambda a: a[0], items)))
    return lax.map(function, items)


def body(inputs, input_proj, readout, step_size, decay_rate, out_grad):
    group_count = input_proj.shape[1] // D_STATE
    blocks = to_spans(
        inputs, out_grad, input_proj, readout, step_size, group_count, D_STATE, HEAD_DIM, SPAN
    )
    rate_rows = decay_rate.reshape(group_count, -1)
    totals, forward, backward = over_spans(lambda e: summarize(*e, rate_rows), blocks)
    if totals.shape[0] == 1:
        device_log, device_fwd, device_bwd = totals[0], forward[0], backward[0]
        log_before = log_after = jnp.zeros_like(totals)
        fwd_before = bwd_after = jnp.zeros_like(forward)
    else:
        (device_log, device_fwd), (log_before, fwd_before) = span_prefix(totals, forward, False)
        (ignored_log, device_bwd), (log_after, bwd_after) = span_prefix(totals, backward, True)
    local = over_spans(lambda e: span_local(*e, rate_rows), blocks)
    device_in, device_out = seq_scan(device_log, device_fwd, device_bwd, "seq")
    state_ins = fwd_before + jnp.exp(log_before)[:, :, None, :, None] * device_in[None]
    grad_ins = bwd_after + jnp.exp(log_after)[:, :, None, :, None] * device_out[None]
    gradients = over_spans(
        lambda e: span_state(*e[0], rate_rows, e[1], e[2], e[3]),
        (blocks, state_ins, grad_ins, local),
    )
    tokens = gradients[0].shape[0] * gradients[0].shape[1]
    grad_inputs, grad_proj, grad_read, grad_step = (g.reshape(tokens, -1) for g in gradients)
    regrouped = lax.all_to_all(grad_step, "tp", split_axis=0, concat_axis=1, tiled=True)
    return (
        grad_inputs.astype(jnp.bfloat16),
        grad_proj.astype(jnp.bfloat16),
        grad_read.astype(jnp.bfloat16),
        regrouped,
    )


def solution(mesh):
    in_specs = (
        P("seq", "tp"),
        P("seq", "tp"),
        P("seq", "tp"),
        P("seq", "tp"),
        P("tp"),
        P("seq", "tp"),
    )
    out_specs = (P("seq", "tp"), P("seq", "tp"), P("seq", "tp"), P(("seq", "tp"), None))
    return jax.shard_map(body, mesh=mesh, in_specs=in_specs, out_specs=out_specs, check_vma=False)
```
